512 devices in a mesh: req: 64 (over z, x, core), tp: 8 (over y).
Axes of the slice: x: 4, y: 8, z: 8, core: 2. Of those that a mesh axis runs over, the one named last changes fastest.
Arguments:
- queries: bfloat16 [16384, 7168], P('req', 'tp'), may hold values from -200 to 200
- key_value: bfloat16 [2, 16384, 1024], P(None, 'req', 'tp'), may hold values from -8 to 8
- segment: int32 [16384], P('req'), may hold values from 0 to 31, never falling along the last dimension, each value on 1 to 1024 neighbouring positions
- residual: bfloat16 [16384, 7168], P('req', 'tp'), may hold values from -4 to 4
- out_weight: bfloat16 [7168, 7168], P('tp', 'req'), may hold values from -0.0625 to 0.0625
- head_gain: bfloat16 [7168], P('tp'), may hold values from 0.099609375 to 1.8984375
- vocab_weight: bfloat16 [7168, 64000], P('tp', 'req'), may hold values from -0.21875 to 0.21875
Outputs:
- hidden: bfloat16 [16384, 7168], P('req', 'tp')
- key_cache: bfloat16 [16384, 1024], P('req', 'tp')
- last_norm: float32 [32], replicated
- top_logit: float32 [32], replicated
The draws below stay inside these ranges and needn't reach their ends.
Inputs may be any that keep to these rules, and one draw needn't show every extreme that they name: `segment`: ids never fall; each of the 32 requests has 1 to 1024 tokens, one has exactly 1024.
All inputs are finite; a program needn't handle non-finite values.
Results may differ from the reference program's by a relative error of at most 0.013.
Values may be sent and summed in bfloat16 or wider, within the bound.
No kernel may reach another device: no remote copies, remote signals or barrier semaphores. Data moves between devices by JAX's collectives and lax.ppermute only.
A program may use at most 128 MiB of HBM per device.

```python
import math
import jax
import jax.numpy as jnp
import numpy as np
from jax import lax

D = 7168
HD = 128
KVH = 8
GROUP = 7
V = 64000
TOK_DEV = 256
QH = 56
TOKENS = 16384
LMAX = 1024
REQS = 32
N_TP = 8


def base_draw(key, salt, shape):
    return jnp.clip(jax.random.normal(jax.random.fold_in(key, salt), shape, jnp.float32), -6.0, 6.0)


def pair_keys(key):
    base = base_draw(key, 21, (TOKENS, KVH, HD))
    return base


def draw_key_value(key, part):
    keys_part = pair_keys(key).reshape(TOKENS, KVH * HD)
    values_part = base_draw(key, 23, (TOKENS, KVH * HD))
    return jnp.stack([keys_part, values_part]).astype(jnp.bfloat16)


def draw_queries(key, part):
    base = base_draw(key, 24, (TOKENS, KVH, GROUP, HD))
    return base.reshape(TOKENS, QH * HD).astype(jnp.bfloat16)


def steps_of(rng, dims, shards, least, top_value):
    loudness, own = 1.0, jax.random.fold_in(rng, 6)
    for axis_at, shards_of in shards:
        draws = jnp.exp(jax.random.uniform(jax.random.fold_in(own, axis_at), (shards_of,), jnp.float32, least / len(shards), top_value / len(shards)))
        loudness = loudness * jnp.repeat(draws, dims[axis_at] // shards_of).reshape([-1 if axis == axis_at else 1 for axis in range(len(dims))])
    return loudness


def profile(count, total, most, lean):
    weights = [(1 << 20) // math.isqrt(standing ** lean) + 1 for standing in range(2, count + 1)]
    surplus, given = total - most - (count - 1), [1] * (count - 1)
    while surplus > 0:
        movable = [i for i in range(count - 1) if given[i] < most]
        whole, remaining = sum([weights[i] for i in movable]), surplus
        for i in movable:
            extra = min(most - given[i], max(1, remaining * weights[i] // whole), surplus)
            given[i] = given[i] + extra
            surplus = surplus - extra
    return np.array([most] + given)


def uneven_parts(rng, amount, total, reach, lean):
    if amount == 2:
        one = jax.random.randint(rng, (), max(1, total - reach), min(reach, total - 1) + 1)
        return jnp.stack([one, total - one])
    sizes = jnp.asarray(profile(amount, total, reach, lean), jnp.int32)
    twos = (amount - 1) // 2
    donor, taker = sizes[1:1 + 2 * twos:2], sizes[2:2 + 2 * twos:2]
    margin = jnp.minimum(donor - 1, reach - taker)
    passed = jax.random.randint(jax.random.fold_in(rng, 1), (twos,), 0, 1 << 20) % (margin + 1)
    sizes = sizes.at[1:1 + 2 * twos:2].set(donor - passed).at[2:2 + 2 * twos:2].set(taker + passed)
    return sizes[jax.random.permutation(jax.random.fold_in(rng, 2), amount)]


def normal_values(own_key, extent, scale, most, split=(), held_as=jnp.bfloat16):
    entries = jax.random.normal(own_key, extent, jnp.float32) * scale
    if len(split) > 0:
        entries = steps_of(own_key, extent, split, -0.22, 0.18) * entries
    return jnp.clip(entries, min=-most, max=most).astype(held_as)


def setup_inputs(seed: int = 0) -> dict:
    arg_keys = jax.random.split(jax.random.key(seed), 8)
    queries = draw_queries(jax.random.fold_in(arg_keys[7], 71), 0)
    key_value = draw_key_value(jax.random.fold_in(arg_keys[7], 71), 0)
    segment = jnp.searchsorted(jnp.cumsum(uneven_parts(arg_keys[2], REQS, TOKENS, LMAX, 2)), jnp.arange(TOKENS), side="right").astype(jnp.int32)
    residual = normal_values(arg_keys[3], (TOKENS, D), 0.3, 4.0, ((0, 64), (1, 8)))
    out_weight = normal_values(arg_keys[4], (QH * HD, D), (QH * HD) ** -0.5, 0.0625, ((0, 8), (1, 64)))
    head_gain = jnp.clip(1.0 + 0.18 * jax.random.normal(arg_keys[5], (D,), jnp.float32), 0.099609375, 1.8984375).astype(jnp.bfloat16)
    vocab_weight = normal_values(arg_keys[6], (D, V), (D // 9) ** -0.5, 0.21875, ((0, 8), (1, 64)))
    return {"queries": queries, "key_value": key_value, "segment": segment, "residual": residual, "out_weight": out_weight, "head_gain": head_gain, "vocab_weight": vocab_weight}


theta = 5000000.0
eps = 1e-05
masked_score = -1e+30

def rope_tables(positions, width):
    half_width = width // 2
    frequency = theta ** (-(jnp.arange(half_width, dtype=jnp.float32) * 2.0 / width))
    angles = positions[:, None] * frequency[None, :]
    return (jnp.cos(angles), jnp.sin(angles))

def rotate(values, cosine, sine_table):
    half_width = values.shape[-1] // 2
    first_half = values[..., :half_width]
    second_half = values[..., half_width:]
    table_shape = (cosine.shape[0],) + (1,) * (values.ndim - 2) + (half_width,)
    cosine = cosine.reshape(table_shape)
    sine_table = sine_table.reshape(table_shape)
    return jnp.concatenate([first_half * cosine - second_half * sine_table, second_half * cosine + first_half * sine_table], axis=-1)

def reference(queries, key_value, segment, residual, out_weight, head_gain, vocab_weight):
    request_ids = jnp.arange(REQS, dtype=jnp.int32)
    member = segment[:, None] == request_ids[None, :]
    lengths = lax.optimization_barrier(jnp.sum(member.astype(jnp.float32), axis=0))
    starts = jnp.cumsum(lengths) - lengths
    tok_index = jnp.arange(TOKENS, dtype=jnp.int32).astype(jnp.float32)
    own_start = lax.optimization_barrier(jnp.sum(jnp.where(member, starts[None, :], 0.0), axis=1))
    positions = tok_index - own_start
    cosine, sine_table = rope_tables(positions, HD)
    rot_query = rotate(queries.astype(jnp.float32).reshape(TOKENS, KVH, GROUP, HD), cosine, sine_table).astype(jnp.bfloat16)
    rot_key = rotate(key_value[0].astype(jnp.float32).reshape(TOKENS, KVH, HD), cosine, sine_table).astype(jnp.bfloat16)
    key_cache = rot_key.reshape(TOKENS, KVH * HD)
    value_rows = key_value[1].reshape(TOKENS, KVH, HD)
    pad_keys = jnp.concatenate([jnp.zeros((LMAX, KVH, HD), jnp.bfloat16), rot_key], axis=0)
    pad_values = jnp.concatenate([jnp.zeros((LMAX, KVH, HD), jnp.bfloat16), value_rows], axis=0)
    span = LMAX + TOK_DEV
    scale = HD ** (-0.5)

    def attend_block(block):
        low = block * TOK_DEV
        q_block = lax.dynamic_slice_in_dim(rot_query, low, TOK_DEV, 0)
        k_block = lax.dynamic_slice_in_dim(pad_keys, low, span, 0)
        v_block = lax.dynamic_slice_in_dim(pad_values, low, span, 0)
        q_index = lax.dynamic_slice_in_dim(tok_index, low, TOK_DEV, 0)
        q_start = lax.dynamic_slice_in_dim(own_start, low, TOK_DEV, 0)
        k_index = (low - LMAX).astype(jnp.float32) + jnp.arange(span, dtype=jnp.float32)
        allowed = (k_index[None, :] >= q_start[:, None]) & (k_index[None, :] <= q_index[:, None])
        scores = jnp.einsum('qhgd,khd->hgqk', q_block.astype(jnp.float32), k_block.astype(jnp.float32)) * scale
        scores = jnp.where(allowed[None, None], scores, masked_score)
        peak = lax.optimization_barrier(jnp.max(scores, axis=3, keepdims=True))
        weights = jnp.exp(scores - peak)
        total = lax.optimization_barrier(jnp.sum(weights, axis=3))
        rounded = lax.optimization_barrier(weights.astype(jnp.bfloat16)).astype(jnp.float32)
        context = jnp.einsum('hgqk,khd->qhgd', rounded, v_block.astype(jnp.float32))
        context = context / jnp.transpose(total, (2, 0, 1))[..., None]
        return context.astype(jnp.bfloat16).reshape(TOK_DEV, QH * HD)
    attended = lax.map(attend_block, jnp.arange(TOKENS // TOK_DEV, dtype=jnp.int32)).reshape(TOKENS, QH * HD)
    share = QH * HD // N_TP
    projected = jnp.zeros((TOKENS, D), jnp.float32)
    for rank in range(N_TP):
        part_sum = jnp.dot(attended[:, rank * share:(rank + 1) * share], out_weight[rank * share:(rank + 1) * share], preferred_element_type=jnp.float32)
        projected = projected + lax.optimization_barrier(part_sum.astype(jnp.bfloat16)).astype(jnp.float32)
    hidden = (residual.astype(jnp.float32) + projected).astype(jnp.bfloat16)
    ends = (starts + lengths - 1.0).astype(jnp.int32)
    last_state = hidden[ends].astype(jnp.float32)
    mean_square = lax.optimization_barrier(jnp.sum(last_state * last_state, axis=1)) / D
    last_norm = jnp.sqrt(mean_square)
    scaled = (last_state * head_gain.astype(jnp.float32)).astype(jnp.bfloat16)
    raw = jnp.dot(scaled, vocab_weight, preferred_element_type=jnp.float32)
    top_logit = lax.optimization_barrier(jnp.max(raw * lax.rsqrt(mean_square + eps)[:, None], axis=1))
    return (hidden, key_cache, last_norm, top_logit)
```

```python
import jax
import jax.numpy as jnp
from jax import lax
from jax.sharding import PartitionSpec as P

D = 7168
HD = 128
GROUP = 7
REACH = 4


theta = 5000000.0
eps = 1e-05
masked_score = -1e30


def from_behind(value, axis, steps):
    count = lax.axis_size(axis)
    initial, last = (max(0, -steps), min(count, count - steps))
    return lax.ppermute(value, axis, [(source, source + steps) for source in range(initial, last)])


def butterfly(value, axis, combine):
    count = lax.axis_size(axis)
    stride = 1
    while stride < count:
        other = lax.ppermute(value, axis, [(source, source ^ stride) for source in range(count)])
        value = combine(value, other)
        stride *= 2
    return value


def rope_tables(positions, width):
    half_width = width // 2
    frequency = theta ** (-(jnp.arange(half_width, dtype=jnp.float32) * 2.0 / width))
    angles = positions[:, None] * frequency[None, :]
    return (jnp.cos(angles), jnp.sin(angles))


def rotate(values, cosine, sine_table):
    half_width = values.shape[-1] // 2
    first_half = values[..., :half_width]
    second_half = values[..., half_width:]
    table_shape = (cosine.shape[0],) + (1,) * (values.ndim - 2) + (half_width,)
    cosine = cosine.reshape(table_shape)
    sine_table = sine_table.reshape(table_shape)
    return jnp.concatenate(
        [
            first_half * cosine - second_half * sine_table,
            second_half * cosine + first_half * sine_table,
        ],
        axis=-1,
    )


def local(queries, key_value, segment, residual, out_weight, head_gain, vocab_weight):
    tok_rows = segment.shape[0]
    heads_kv = key_value.shape[2] // HD
    requests = lax.axis_size("req") // 2
    devices_req = lax.axis_size("req")
    device = lax.axis_index("req")
    request_ids = jnp.arange(requests, dtype=jnp.int32)

    own_kv = key_value
    parts_kv, parts_seg = [], []
    for back in range(REACH, 0, -1):
        kv_b, seg_b = from_behind((own_kv, segment), "req", back)
        parts_kv.append(kv_b)
        parts_seg.append(seg_b)
    parts_kv.append(own_kv)
    parts_seg.append(segment)
    next_first = from_behind(segment[:1], "req", -1)
    window = jnp.concatenate(parts_kv, axis=1)
    seg_window = jnp.concatenate(parts_seg, axis=0)
    span = window.shape[1]
    key_index_i = (device - REACH) * tok_rows + jnp.arange(span, dtype=jnp.int32)
    valid = key_index_i >= 0
    same = (seg_window[:, None] == seg_window[None, :]) & valid[None, :]
    start_i = jnp.min(jnp.where(same, key_index_i[None, :], jnp.int32(2**30)), axis=1)
    key_index = key_index_i.astype(jnp.float32)
    win_start = start_i.astype(jnp.float32)
    win_pos = key_index - win_start
    own_start = win_start[span - tok_rows:]
    tok_index = key_index[span - tok_rows:]
    positions = win_pos[span - tok_rows:]

    cosine, sine_table = rope_tables(win_pos, HD)
    rot_keys = rotate(
        window[0].astype(jnp.float32).reshape(span, heads_kv, HD), cosine, sine_table
    ).astype(jnp.bfloat16)
    q_cos, q_sin = cosine[span - tok_rows:], sine_table[span - tok_rows:]
    rot_query = rotate(
        queries.astype(jnp.float32).reshape(tok_rows, heads_kv, GROUP, HD), q_cos, q_sin
    ).astype(jnp.bfloat16)
    key_cache = rot_keys[span - tok_rows:].reshape(tok_rows, heads_kv * HD)
    key_rows = rot_keys
    value_rows = window[1].reshape(span, heads_kv, HD)
    q_seg = segment
    allowed = (
        (seg_window[None, :] == q_seg[:, None])
        & valid[None, :]
        & (key_index[None, :] <= tok_index[:, None])
    )
    scale = HD ** (-0.5)
    scores_part = (
        jnp.einsum("qhgd,khd->hgqk", rot_query, key_rows, preferred_element_type=jnp.float32)
        * scale
    )
    scores = jnp.where(allowed[None, None], scores_part, masked_score)
    peak = jnp.max(scores, axis=3, keepdims=True)
    weights = jnp.exp(scores - peak)
    total = jnp.sum(weights, axis=3)
    context = jnp.einsum(
        "hgqk,khd->qhgd",
        weights.astype(jnp.bfloat16),
        value_rows,
        preferred_element_type=jnp.float32,
    )
    context = context / jnp.transpose(total, (2, 0, 1))[..., None]
    attended = context.astype(jnp.bfloat16).reshape(tok_rows, heads_kv * GROUP * HD)
    projected = jnp.dot(
        attended,
        lax.all_gather(out_weight, "req", axis=1, tiled=True),
        preferred_element_type=jnp.float32,
    )
    own_share = lax.psum_scatter(
        projected.astype(jnp.bfloat16), "tp", scatter_dimension=1, tiled=True
    ).astype(jnp.float32)
    hidden = (residual.astype(jnp.float32) + own_share).astype(jnp.bfloat16)

    following = jnp.concatenate([segment[1:], next_first])
    is_last_dev = device == devices_req - 1
    is_end = following != segment
    is_end = is_end.at[tok_rows - 1].set(is_end[tok_rows - 1] | is_last_dev)
    select = (is_end[:, None] & (segment[:, None] == request_ids[None, :])).astype(jnp.bfloat16)
    local_last = lax.dot_general(
        select, hidden, (((0,), (0,)), ((), ())), preferred_element_type=jnp.float32
    )
    last_state = butterfly(local_last.astype(jnp.bfloat16), "req", jnp.add).astype(jnp.float32)
    scaled = (last_state * head_gain.astype(jnp.float32)).astype(jnp.bfloat16)
    square_part = jnp.sum(last_state * last_state, axis=1)
    logit_part = jnp.dot(scaled, vocab_weight, preferred_element_type=jnp.float32)
    square_sum, raw_logits = (
        lax.psum(square_part.astype(jnp.bfloat16), "tp").astype(jnp.float32),
        lax.psum(logit_part.astype(jnp.bfloat16), "tp").astype(jnp.float32),
    )
    mean_square = square_sum / D
    last_norm = jnp.sqrt(mean_square)
    local_top = jnp.max(raw_logits * lax.rsqrt(mean_square + eps)[:, None], axis=1)
    top_logit = butterfly(local_top, "req", jnp.maximum)
    return (hidden, key_cache, last_norm, top_logit)


def solution(mesh):
    placed = (
        P("req", "tp"),
        P(None, "req", "tp"),
        P("req"),
        P("req", "tp"),
        P("tp", "req"),
        P("tp"),
        P("tp", "req"),
    )
    return jax.shard_map(
        local,
        mesh=mesh,
        in_specs=placed,
        out_specs=(P("req", "tp"), P("req", "tp"), P(), P()),
        check_vma=False,
    )
```

```python
import jax
import jax.numpy as jnp
from jax import lax
from jax.sharding import PartitionSpec as P

D = 7168
HD = 128
GROUP = 7
REACH = 4


theta = 5000000.0
eps = 1e-05
masked_score = -1e30


def from_behind(value, axis, steps):
    count = lax.axis_size(axis)
    initial, last = (max(0, -steps), min(count, count - steps))
    return lax.ppermute(value, axis, [(source, source + steps) for source in range(initial, last)])


def butterfly(value, axis, combine):
    count = lax.axis_size(axis)
    stride = 1
    while stride < count:
        other = lax.ppermute(value, axis, [(source, source ^ stride) for source in range(count)])
        value = combine(value, other)
        stride *= 2
    return value


def halving_scatter(value, axis):
    count = lax.axis_size(axis)
    index = lax.axis_index(axis)
    rows = value.shape[0]
    held = value.reshape(rows, count, value.shape[1] // count)
    bit = count // 2
    while bit >= 1:
        half = held.shape[1] // 2
        mine = (index // bit) % 2
        keep = lax.dynamic_slice_in_dim(held, mine * half, half, 1)
        give = lax.dynamic_slice_in_dim(held, (1 - mine) * half, half, 1)
        held = keep + lax.ppermute(give, axis, [(source, source ^ bit) for source in range(count)])
        bit //= 2
    return held.reshape(rows, -1)


def rope_tables(positions, width):
    half_width = width // 2
    frequency = theta ** (-(jnp.arange(half_width, dtype=jnp.float32) * 2.0 / width))
    angles = positions[:, None] * frequency[None, :]
    return (jnp.cos(angles), jnp.sin(angles))


def rotate(values, cosine, sine_table):
    half_width = values.shape[-1] // 2
    first_half = values[..., :half_width]
    second_half = values[..., half_width:]
    table_shape = (cosine.shape[0],) + (1,) * (values.ndim - 2) + (half_width,)
    cosine = cosine.reshape(table_shape)
    sine_table = sine_table.reshape(table_shape)
    return jnp.concatenate(
        [
            first_half * cosine - second_half * sine_table,
            second_half * cosine + first_half * sine_table,
        ],
        axis=-1,
    )


def local(queries, key_value, segment, residual, out_weight, head_gain, vocab_weight):
    tok_rows = segment.shape[0]
    heads_kv = key_value.shape[2] // HD
    requests = lax.axis_size("req") // 2
    devices_req = lax.axis_size("req")
    device = lax.axis_index("req")
    request_ids = jnp.arange(requests, dtype=jnp.int32)

    own_kv = key_value
    parts_kv, parts_seg = [], []
    for back in range(REACH, 0, -1):
        kv_b, seg_b = from_behind((own_kv, segment), "req", back)
        parts_kv.append(kv_b)
        parts_seg.append(seg_b)
    parts_kv.append(own_kv)
    parts_seg.append(segment)
    next_first = from_behind(segment[:1], "req", -1)
    window = jnp.concatenate(parts_kv, axis=1)
    seg_window = jnp.concatenate(parts_seg, axis=0)
    span = window.shape[1]
    key_index_i = (device - REACH) * tok_rows + jnp.arange(span, dtype=jnp.int32)
    valid = key_index_i >= 0
    same = (seg_window[:, None] == seg_window[None, :]) & valid[None, :]
    start_i = jnp.min(jnp.where(same, key_index_i[None, :], jnp.int32(2**30)), axis=1)
    key_index = key_index_i.astype(jnp.float32)
    win_start = start_i.astype(jnp.float32)
    win_pos = key_index - win_start
    own_start = win_start[span - tok_rows:]
    tok_index = key_index[span - tok_rows:]
    positions = win_pos[span - tok_rows:]

    cosine, sine_table = rope_tables(win_pos, HD)
    rot_keys = rotate(
        window[0].astype(jnp.float32).reshape(span, heads_kv, HD), cosine, sine_table
    ).astype(jnp.bfloat16)
    q_cos, q_sin = cosine[span - tok_rows:], sine_table[span - tok_rows:]
    rot_query = rotate(
        queries.astype(jnp.float32).reshape(tok_rows, heads_kv, GROUP, HD), q_cos, q_sin
    ).astype(jnp.bfloat16)
    key_cache = rot_keys[span - tok_rows:].reshape(tok_rows, heads_kv * HD)
    key_rows = rot_keys
    value_rows = window[1].reshape(span, heads_kv, HD)
    q_seg = segment
    allowed = (
        (seg_window[None, :] == q_seg[:, None])
        & valid[None, :]
        & (key_index[None, :] <= tok_index[:, None])
    )
    scale = HD ** (-0.5)
    scores_part = (
        jnp.einsum("qhgd,khd->hgqk", rot_query, key_rows, preferred_element_type=jnp.float32)
        * scale
    )
    scores = jnp.where(allowed[None, None], scores_part, masked_score)
    peak = jnp.max(scores, axis=3, keepdims=True)
    weights = jnp.exp(scores - peak)
    total = jnp.sum(weights, axis=3)
    context = jnp.einsum(
        "hgqk,khd->qhgd",
        weights.astype(jnp.bfloat16),
        value_rows,
        preferred_element_type=jnp.float32,
    )
    context = context / jnp.transpose(total, (2, 0, 1))[..., None]
    attended = context.astype(jnp.bfloat16).reshape(tok_rows, heads_kv * GROUP * HD)
    following = jnp.concatenate([segment[1:], next_first])
    is_last_dev = device == devices_req - 1
    is_end = following != segment
    is_end = is_end.at[tok_rows - 1].set(is_end[tok_rows - 1] | is_last_dev)
    select = (is_end[:, None] & (segment[:, None] == request_ids[None, :])).astype(jnp.bfloat16)
    end_rows = lax.dot_general(
        select,
        jnp.concatenate([attended, residual], axis=1),
        (((0,), (0,)), ((), ())),
        preferred_element_type=jnp.float32,
    ).astype(jnp.bfloat16)
    end_rows = butterfly(end_rows, "req", jnp.add)
    end_att, end_res = end_rows[:, : attended.shape[1]], end_rows[:, attended.shape[1] :]

    full_weight = lax.all_gather(out_weight, "req", axis=1, tiled=True)
    projected = jnp.dot(attended, full_weight, preferred_element_type=jnp.float32)
    own_share = lax.psum_scatter(
        projected.astype(jnp.bfloat16), "tp", scatter_dimension=1, tiled=True
    ).astype(jnp.float32)
    hidden = (residual.astype(jnp.float32) + own_share).astype(jnp.bfloat16)

    end_part = jnp.dot(end_att, full_weight, preferred_element_type=jnp.float32)
    end_part = end_part.astype(jnp.bfloat16).astype(jnp.float32)
    end_sum = halving_scatter(end_part, "tp")
    last_state = (end_res.astype(jnp.float32) + end_sum).astype(jnp.bfloat16).astype(jnp.float32)
    scaled = (last_state * head_gain.astype(jnp.float32)).astype(jnp.bfloat16)
    square_part = jnp.sum(last_state * last_state, axis=1)
    logit_part = jnp.dot(scaled, vocab_weight, preferred_element_type=jnp.float32)
    summed = butterfly(
        jnp.concatenate([logit_part, square_part[:, None]], axis=1), "tp", jnp.add
    )
    raw_logits, square_sum = summed[:, :-1], summed[:, -1]
    mean_square = square_sum / D
    last_norm = jnp.sqrt(mean_square)
    local_top = jnp.max(raw_logits * lax.rsqrt(mean_square + eps)[:, None], axis=1)
    top_logit = butterfly(local_top, "req", jnp.maximum)
    return (hidden, key_cache, last_norm, top_logit)


def solution(mesh):
    placed = (
        P("req", "tp"),
        P(None, "req", "tp"),
        P("req"),
        P("req", "tp"),
        P("tp", "req"),
        P("tp"),
        P("tp", "req"),
    )
    return jax.shard_map(
        local,
        mesh=mesh,
        in_specs=placed,
        out_specs=(P("req", "tp"), P("req", "tp"), P(), P()),
        check_vma=False,
    )
```

```python
import jax
import jax.numpy as jnp
from jax import lax
from jax.sharding import PartitionSpec as P

D = 7168
HD = 128
GROUP = 7
REACH = 4


theta = 5000000.0
eps = 1e-05
masked_score = -1e30


def from_behind(value, axis, steps):
    count = lax.axis_size(axis)
    initial, last = (max(0, -steps), min(count, count - steps))
    return lax.ppermute(value, axis, [(source, source + steps) for source in range(initial, last)])


def butterfly(value, axis, combine):
    count = lax.axis_size(axis)
    stride = 1
    while stride < count:
        other = lax.ppermute(value, axis, [(source, source ^ stride) for source in range(count)])
        value = combine(value, other)
        stride *= 2
    return value


def halving_scatter(value, axis):
    count = lax.axis_size(axis)
    index = lax.axis_index(axis)
    rows = value.shape[0]
    held = value.reshape(rows, count, value.shape[1] // count)
    bit = count // 2
    while bit >= 1:
        if bit < count // 2:
            held = held.astype(jnp.float32)
        half = held.shape[1] // 2
        mine = (index // bit) % 2
        keep = lax.dynamic_slice_in_dim(held, mine * half, half, 1)
        give = lax.dynamic_slice_in_dim(held, (1 - mine) * half, half, 1)
        held = keep.astype(jnp.float32) + lax.ppermute(give, axis, [(source, source ^ bit) for source in range(count)]).astype(jnp.float32)
        bit //= 2
    return held.reshape(rows, -1)


def rope_tables(positions, width):
    half_width = width // 2
    frequency = theta ** (-(jnp.arange(half_width, dtype=jnp.float32) * 2.0 / width))
    angles = positions[:, None] * frequency[None, :]
    return (jnp.cos(angles), jnp.sin(angles))


def rotate(values, cosine, sine_table):
    half_width = values.shape[-1] // 2
    first_half = values[..., :half_width]
    second_half = values[..., half_width:]
    table_shape = (cosine.shape[0],) + (1,) * (values.ndim - 2) + (half_width,)
    cosine = cosine.reshape(table_shape)
    sine_table = sine_table.reshape(table_shape)
    return jnp.concatenate(
        [
            first_half * cosine - second_half * sine_table,
            second_half * cosine + first_half * sine_table,
        ],
        axis=-1,
    )


def local(queries, key_value, segment, residual, out_weight, head_gain, vocab_weight):
    tok_rows = segment.shape[0]
    heads_kv = key_value.shape[2] // HD
    requests = lax.axis_size("req") // 2
    devices_req = lax.axis_size("req")
    device = lax.axis_index("req")
    request_ids = jnp.arange(requests, dtype=jnp.int32)

    own_kv = key_value
    parts_kv, parts_seg = [], []
    for back in range(REACH, 0, -1):
        kv_b, seg_b = from_behind((own_kv, segment), "req", back)
        parts_kv.append(kv_b)
        parts_seg.append(seg_b)
    parts_kv.append(own_kv)
    parts_seg.append(segment)
    next_first = from_behind(segment[:1], "req", -1)
    window = jnp.concatenate(parts_kv, axis=1)
    seg_window = jnp.concatenate(parts_seg, axis=0)
    span = window.shape[1]
    key_index_i = (device - REACH) * tok_rows + jnp.arange(span, dtype=jnp.int32)
    valid = key_index_i >= 0
    same = (seg_window[:, None] == seg_window[None, :]) & valid[None, :]
    start_i = jnp.min(jnp.where(same, key_index_i[None, :], jnp.int32(2**30)), axis=1)
    key_index = key_index_i.astype(jnp.float32)
    win_start = start_i.astype(jnp.float32)
    win_pos = key_index - win_start
    own_start = win_start[span - tok_rows:]
    tok_index = key_index[span - tok_rows:]
    positions = win_pos[span - tok_rows:]

    cosine, sine_table = rope_tables(win_pos, HD)
    rot_keys = rotate(
        window[0].astype(jnp.float32).reshape(span, heads_kv, HD), cosine, sine_table
    ).astype(jnp.bfloat16)
    q_cos, q_sin = cosine[span - tok_rows:], sine_table[span - tok_rows:]
    rot_query = rotate(
        queries.astype(jnp.float32).reshape(tok_rows, heads_kv, GROUP, HD), q_cos, q_sin
    ).astype(jnp.bfloat16)
    key_cache = rot_keys[span - tok_rows:].reshape(tok_rows, heads_kv * HD)
    key_rows = rot_keys
    value_rows = window[1].reshape(span, heads_kv, HD)
    q_seg = segment
    allowed = (
        (seg_window[None, :] == q_seg[:, None])
        & valid[None, :]
        & (key_index[None, :] <= tok_index[:, None])
    )
    scale = HD ** (-0.5)
    scores_part = (
        jnp.einsum("qhgd,khd->hgqk", rot_query, key_rows, preferred_element_type=jnp.float32)
        * scale
    )
    scores = jnp.where(allowed[None, None], scores_part, masked_score)
    peak = jnp.max(scores, axis=3, keepdims=True)
    weights = jnp.exp(scores - peak)
    total = jnp.sum(weights, axis=3)
    context = jnp.einsum(
        "hgqk,khd->qhgd",
        weights.astype(jnp.bfloat16),
        value_rows,
        preferred_element_type=jnp.float32,
    )
    context = context / jnp.transpose(total, (2, 0, 1))[..., None]
    attended = context.astype(jnp.bfloat16).reshape(tok_rows, heads_kv * GROUP * HD)
    following = jnp.concatenate([segment[1:], next_first])
    is_last_dev = device == devices_req - 1
    is_end = following != segment
    is_end = is_end.at[tok_rows - 1].set(is_end[tok_rows - 1] | is_last_dev)
    select = (is_end[:, None] & (segment[:, None] == request_ids[None, :])).astype(jnp.bfloat16)
    end_rows = lax.dot_general(
        select,
        jnp.concatenate([attended, residual], axis=1),
        (((0,), (0,)), ((), ())),
        preferred_element_type=jnp.float32,
    ).astype(jnp.bfloat16)
    end_rows = butterfly(end_rows, "req", jnp.add)
    attended, end_rows = lax.optimization_barrier((attended, end_rows))
    end_att, end_res = end_rows[:, : attended.shape[1]], end_rows[:, attended.shape[1] :]

    full_weight = lax.all_gather(out_weight, "req", axis=1, tiled=True)
    end_part = jnp.dot(end_att, full_weight, preferred_element_type=jnp.float32)
    end_part = end_part.astype(jnp.bfloat16)
    attended, end_part = lax.optimization_barrier((attended, end_part))
    projected = jnp.dot(attended, full_weight, preferred_element_type=jnp.float32)
    own_share = lax.psum_scatter(
        projected.astype(jnp.bfloat16), "tp", scatter_dimension=1, tiled=True
    ).astype(jnp.float32)
    hidden = (residual.astype(jnp.float32) + own_share).astype(jnp.bfloat16)

    end_sum = halving_scatter(end_part, "tp")
    last_state = (end_res.astype(jnp.float32) + end_sum).astype(jnp.bfloat16).astype(jnp.float32)
    scaled = (last_state * head_gain.astype(jnp.float32)).astype(jnp.bfloat16)
    square_part = jnp.sum(last_state * last_state, axis=1)
    logit_part = jnp.dot(scaled, vocab_weight, preferred_element_type=jnp.float32)
    summed = butterfly(
        jnp.concatenate([logit_part, square_part[:, None]], axis=1), "tp", jnp.add
    )
    raw_logits, square_sum = summed[:, :-1], summed[:, -1]
    mean_square = square_sum / D
    last_norm = jnp.sqrt(mean_square)
    local_top = jnp.max(raw_logits * lax.rsqrt(mean_square + eps)[:, None], axis=1)
    top_logit = butterfly(local_top, "req", jnp.maximum)
    return (hidden, key_cache, last_norm, top_logit)


def solution(mesh):
    placed = (
        P("req", "tp"),
        P(None, "req", "tp"),
        P("req"),
        P("req", "tp"),
        P("tp", "req"),
        P("tp"),
        P("tp", "req"),
    )
    return jax.shard_map(
        local,
        mesh=mesh,
        in_specs=placed,
        out_specs=(P("req", "tp"), P("req", "tp"), P(), P()),
        check_vma=False,
    )
```

```python
import jax
import jax.numpy as jnp
from jax import lax
from jax.sharding import PartitionSpec as P

D = 7168
HD = 128
GROUP = 7
REACH = 4


theta = 5000000.0
eps = 1e-05
masked_score = -1e30


def from_behind(value, axis, steps):
    count = lax.axis_size(axis)
    initial, last = (max(0, -steps), min(count, count - steps))
    return lax.ppermute(value, axis, [(source, source + steps) for source in range(initial, last)])


def butterfly(value, axis, combine):
    count = lax.axis_size(axis)
    stride = 1
    while stride < count:
        other = lax.ppermute(value, axis, [(source, source ^ stride) for source in range(count)])
        value = combine(value, other)
        stride *= 2
    return value


def direct_scatter(value, axis):
    count = lax.axis_size(axis)
    index = lax.axis_index(axis)
    rows = value.shape[0]
    held = value.reshape(rows, count, value.shape[1] // count)
    total = lax.dynamic_index_in_dim(held, index, 1, keepdims=False).astype(jnp.float32)
    for shift in range(1, count):
        piece = lax.dynamic_index_in_dim(held, (index + shift) % count, 1, keepdims=False)
        moved = lax.ppermute(piece, axis, [(source, (source + shift) % count) for source in range(count)])
        total = total + moved.astype(jnp.float32)
    return total


def direct_sum(value, axis):
    count = lax.axis_size(axis)
    index = lax.axis_index(axis)
    pieces = [value]
    for shift in range(1, count):
        pieces.append(
            lax.ppermute(value, axis, [(source, (source + shift) % count) for source in range(count)])
        )
    stacked = jnp.stack(pieces)
    by_source = jnp.take(stacked, (index - jnp.arange(count)) % count, axis=0)
    return jnp.sum(by_source, axis=0)


def rope_tables(positions, width):
    half_width = width // 2
    frequency = theta ** (-(jnp.arange(half_width, dtype=jnp.float32) * 2.0 / width))
    angles = positions[:, None] * frequency[None, :]
    return (jnp.cos(angles), jnp.sin(angles))


def rotate(values, cosine, sine_table):
    half_width = values.shape[-1] // 2
    first_half = values[..., :half_width]
    second_half = values[..., half_width:]
    table_shape = (cosine.shape[0],) + (1,) * (values.ndim - 2) + (half_width,)
    cosine = cosine.reshape(table_shape)
    sine_table = sine_table.reshape(table_shape)
    return jnp.concatenate(
        [
            first_half * cosine - second_half * sine_table,
            second_half * cosine + first_half * sine_table,
        ],
        axis=-1,
    )


def local(queries, key_value, segment, residual, out_weight, head_gain, vocab_weight):
    tok_rows = segment.shape[0]
    heads_kv = key_value.shape[2] // HD
    requests = lax.axis_size("req") // 2
    devices_req = lax.axis_size("req")
    device = lax.axis_index("req")
    request_ids = jnp.arange(requests, dtype=jnp.int32)

    own_kv = key_value
    parts_kv, parts_seg = [], []
    for back in range(REACH, 0, -1):
        kv_b, seg_b = from_behind((own_kv, segment), "req", back)
        parts_kv.append(kv_b)
        parts_seg.append(seg_b)
    parts_kv.append(own_kv)
    parts_seg.append(segment)
    next_first = from_behind(segment[:1], "req", -1)
    window = jnp.concatenate(parts_kv, axis=1)
    seg_window = jnp.concatenate(parts_seg, axis=0)
    span = window.shape[1]
    key_index_i = (device - REACH) * tok_rows + jnp.arange(span, dtype=jnp.int32)
    valid = key_index_i >= 0
    same = (seg_window[:, None] == seg_window[None, :]) & valid[None, :]
    start_i = jnp.min(jnp.where(same, key_index_i[None, :], jnp.int32(2**30)), axis=1)
    key_index = key_index_i.astype(jnp.float32)
    win_start = start_i.astype(jnp.float32)
    win_pos = key_index - win_start
    own_start = win_start[span - tok_rows:]
    tok_index = key_index[span - tok_rows:]
    positions = win_pos[span - tok_rows:]

    cosine, sine_table = rope_tables(win_pos, HD)
    rot_keys = rotate(
        window[0].astype(jnp.float32).reshape(span, heads_kv, HD), cosine, sine_table
    ).astype(jnp.bfloat16)
    q_cos, q_sin = cosine[span - tok_rows:], sine_table[span - tok_rows:]
    rot_query = rotate(
        queries.astype(jnp.float32).reshape(tok_rows, heads_kv, GROUP, HD), q_cos, q_sin
    ).astype(jnp.bfloat16)
    key_cache = rot_keys[span - tok_rows:].reshape(tok_rows, heads_kv * HD)
    key_rows = rot_keys
    value_rows = window[1].reshape(span, heads_kv, HD)
    q_seg = segment
    allowed = (
        (seg_window[None, :] == q_seg[:, None])
        & valid[None, :]
        & (key_index[None, :] <= tok_index[:, None])
    )
    scale = HD ** (-0.5)
    scores_part = (
        jnp.einsum("qhgd,khd->hgqk", rot_query, key_rows, preferred_element_type=jnp.float32)
        * scale
    )
    scores = jnp.where(allowed[None, None], scores_part, masked_score)
    peak = jnp.max(scores, axis=3, keepdims=True)
    weights = jnp.exp(scores - peak)
    total = jnp.sum(weights, axis=3)
    context = jnp.einsum(
        "hgqk,khd->qhgd",
        weights.astype(jnp.bfloat16),
        value_rows,
        preferred_element_type=jnp.float32,
    )
    context = context / jnp.transpose(total, (2, 0, 1))[..., None]
    attended = context.astype(jnp.bfloat16).reshape(tok_rows, heads_kv * GROUP * HD)
    following = jnp.concatenate([segment[1:], next_first])
    is_last_dev = device == devices_req - 1
    is_end = following != segment
    is_end = is_end.at[tok_rows - 1].set(is_end[tok_rows - 1] | is_last_dev)
    select = (is_end[:, None] & (segment[:, None] == request_ids[None, :])).astype(jnp.bfloat16)
    end_rows = lax.dot_general(
        select,
        jnp.concatenate([attended, residual], axis=1),
        (((0,), (0,)), ((), ())),
        preferred_element_type=jnp.float32,
    ).astype(jnp.bfloat16)
    end_rows = butterfly(end_rows, "req", jnp.add)
    attended, end_rows = lax.optimization_barrier((attended, end_rows))
    end_att, end_res = end_rows[:, : attended.shape[1]], end_rows[:, attended.shape[1] :]

    full_weight = lax.all_gather(out_weight, "req", axis=1, tiled=True)
    end_part = jnp.dot(end_att, full_weight, preferred_element_type=jnp.float32)
    end_part = end_part.astype(jnp.bfloat16)
    attended, end_part = lax.optimization_barrier((attended, end_part))
    projected = jnp.dot(attended, full_weight, preferred_element_type=jnp.float32)
    own_share = lax.psum_scatter(
        projected.astype(jnp.bfloat16), "tp", scatter_dimension=1, tiled=True
    ).astype(jnp.float32)
    hidden = (residual.astype(jnp.float32) + own_share).astype(jnp.bfloat16)

    end_sum = direct_scatter(end_part, "tp")
    last_state = (end_res.astype(jnp.float32) + end_sum).astype(jnp.bfloat16).astype(jnp.float32)
    scaled = (last_state * head_gain.astype(jnp.float32)).astype(jnp.bfloat16)
    square_part = jnp.sum(last_state * last_state, axis=1)
    logit_part = jnp.dot(scaled, vocab_weight, preferred_element_type=jnp.float32)
    summed = direct_sum(jnp.concatenate([logit_part, square_part[:, None]], axis=1), "tp")
    raw_logits, square_sum = summed[:, :-1], summed[:, -1]
    mean_square = square_sum / D
    last_norm = jnp.sqrt(mean_square)
    local_top = jnp.max(raw_logits * lax.rsqrt(mean_square + eps)[:, None], axis=1)
    top_logit = butterfly(local_top, "req", jnp.maximum)
    return (hidden, key_cache, last_norm, top_logit)


def solution(mesh):
    placed = (
        P("req", "tp"),
        P(None, "req", "tp"),
        P("req"),
        P("req", "tp"),
        P("tp", "req"),
        P("tp"),
        P("tp", "req"),
    )
    return jax.shard_map(
        local,
        mesh=mesh,
        in_specs=placed,
        out_specs=(P("req", "tp"), P("req", "tp"), P(), P()),
        check_vma=False,
    )
```

```python
import jax
import jax.numpy as jnp
from jax import lax
from jax.sharding import PartitionSpec as P

D = 7168
HD = 128
GROUP = 7
REACH = 4


theta = 5000000.0
eps = 1e-05
masked_score = -1e30


def from_behind(value, axis, steps):
    count = lax.axis_size(axis)
    initial, last = (max(0, -steps), min(count, count - steps))
    return lax.ppermute(value, axis, [(source, source + steps) for source in range(initial, last)])


def butterfly(value, axis, combine):
    count = lax.axis_size(axis)
    stride = 1
    while stride < count:
        other = lax.ppermute(value, axis, [(source, source ^ stride) for source in range(count)])
        value = combine(value, other)
        stride *= 2
    return value


def halving_scatter(value, axis):
    count = lax.axis_size(axis)
    index = lax.axis_index(axis)
    rows = value.shape[0]
    held = value.reshape(rows, count, value.shape[1] // count)
    bit = count // 2
    while bit >= 1:
        if bit < count // 2:
            held = held.astype(jnp.float32)
        half = held.shape[1] // 2
        mine = (index // bit) % 2
        keep = lax.dynamic_slice_in_dim(held, mine * half, half, 1)
        give = lax.dynamic_slice_in_dim(held, (1 - mine) * half, half, 1)
        held = keep.astype(jnp.float32) + lax.ppermute(give, axis, [(source, source ^ bit) for source in range(count)]).astype(jnp.float32)
        bit //= 2
    return held.reshape(rows, -1)


def rope_tables(positions, width):
    half_width = width // 2
    frequency = theta ** (-(jnp.arange(half_width, dtype=jnp.float32) * 2.0 / width))
    angles = positions[:, None] * frequency[None, :]
    return (jnp.cos(angles), jnp.sin(angles))


def rotate(values, cosine, sine_table):
    half_width = values.shape[-1] // 2
    first_half = values[..., :half_width]
    second_half = values[..., half_width:]
    table_shape = (cosine.shape[0],) + (1,) * (values.ndim - 2) + (half_width,)
    cosine = cosine.reshape(table_shape)
    sine_table = sine_table.reshape(table_shape)
    return jnp.concatenate(
        [
            first_half * cosine - second_half * sine_table,
            second_half * cosine + first_half * sine_table,
        ],
        axis=-1,
    )


def local(queries, key_value, segment, residual, out_weight, head_gain, vocab_weight):
    tok_rows = segment.shape[0]
    heads_kv = key_value.shape[2] // HD
    requests = lax.axis_size("req") // 2
    devices_req = lax.axis_size("req")
    device = lax.axis_index("req")
    request_ids = jnp.arange(requests, dtype=jnp.int32)

    own_kv = key_value
    width = own_kv.shape[2]
    seg_rows = -(-tok_rows // width)
    seg_flat = jnp.pad(segment, (0, seg_rows * width - tok_rows)).astype(jnp.bfloat16)
    packed = jnp.concatenate(
        [own_kv.reshape(2 * tok_rows, width), seg_flat.reshape(seg_rows, width)], axis=0
    )
    parts_kv, parts_seg = [], []
    for back in range(REACH, 0, -1):
        got = from_behind(packed, "req", back)
        parts_kv.append(got[: 2 * tok_rows].reshape(own_kv.shape))
        parts_seg.append(got[2 * tok_rows :].reshape(-1)[:tok_rows].astype(jnp.int32))
    parts_kv.append(own_kv)
    parts_seg.append(segment)
    next_first = from_behind(segment[:1], "req", -1)
    window = jnp.concatenate(parts_kv, axis=1)
    seg_window = jnp.concatenate(parts_seg, axis=0)
    span = window.shape[1]
    key_index_i = (device - REACH) * tok_rows + jnp.arange(span, dtype=jnp.int32)
    valid = key_index_i >= 0
    same = (seg_window[:, None] == seg_window[None, :]) & valid[None, :]
    start_i = jnp.min(jnp.where(same, key_index_i[None, :], jnp.int32(2**30)), axis=1)
    key_index = key_index_i.astype(jnp.float32)
    win_start = start_i.astype(jnp.float32)
    win_pos = key_index - win_start
    own_start = win_start[span - tok_rows:]
    tok_index = key_index[span - tok_rows:]
    positions = win_pos[span - tok_rows:]

    cosine, sine_table = rope_tables(win_pos, HD)
    rot_keys = rotate(
        window[0].astype(jnp.float32).reshape(span, heads_kv, HD), cosine, sine_table
    ).astype(jnp.bfloat16)
    q_cos, q_sin = cosine[span - tok_rows:], sine_table[span - tok_rows:]
    rot_query = rotate(
        queries.astype(jnp.float32).reshape(tok_rows, heads_kv, GROUP, HD), q_cos, q_sin
    ).astype(jnp.bfloat16)
    key_cache = rot_keys[span - tok_rows:].reshape(tok_rows, heads_kv * HD)
    key_rows = rot_keys
    value_rows = window[1].reshape(span, heads_kv, HD)
    q_seg = segment
    allowed = (
        (seg_window[None, :] == q_seg[:, None])
        & valid[None, :]
        & (key_index[None, :] <= tok_index[:, None])
    )
    scale = HD ** (-0.5)
    scores_part = (
        jnp.einsum("qhgd,khd->hgqk", rot_query, key_rows, preferred_element_type=jnp.float32)
        * scale
    )
    scores = jnp.where(allowed[None, None], scores_part, masked_score)
    peak = jnp.max(scores, axis=3, keepdims=True)
    weights = jnp.exp(scores - peak)
    total = jnp.sum(weights, axis=3)
    context = jnp.einsum(
        "hgqk,khd->qhgd",
        weights.astype(jnp.bfloat16),
        value_rows,
        preferred_element_type=jnp.float32,
    )
    context = context / jnp.transpose(total, (2, 0, 1))[..., None]
    attended = context.astype(jnp.bfloat16).reshape(tok_rows, heads_kv * GROUP * HD)
    following = jnp.concatenate([segment[1:], next_first])
    is_last_dev = device == devices_req - 1
    is_end = following != segment
    is_end = is_end.at[tok_rows - 1].set(is_end[tok_rows - 1] | is_last_dev)
    select = (is_end[:, None] & (segment[:, None] == request_ids[None, :])).astype(jnp.bfloat16)
    end_rows = lax.dot_general(
        select,
        jnp.concatenate([attended, residual], axis=1),
        (((0,), (0,)), ((), ())),
        preferred_element_type=jnp.float32,
    ).astype(jnp.bfloat16)
    end_rows = butterfly(end_rows, "req", jnp.add)
    attended, end_rows = lax.optimization_barrier((attended, end_rows))
    end_att, end_res = end_rows[:, : attended.shape[1]], end_rows[:, attended.shape[1] :]

    full_weight = lax.all_gather(out_weight, "req", axis=1, tiled=True)
    both = jnp.dot(
        jnp.concatenate([attended, end_att], axis=0), full_weight, preferred_element_type=jnp.float32
    ).astype(jnp.bfloat16)
    projected, end_part = both[:tok_rows], both[tok_rows:]
    own_share = lax.psum_scatter(projected, "tp", scatter_dimension=1, tiled=True).astype(jnp.float32)
    hidden = (residual.astype(jnp.float32) + own_share).astype(jnp.bfloat16)

    end_sum = halving_scatter(end_part, "tp")
    last_state = (end_res.astype(jnp.float32) + end_sum).astype(jnp.bfloat16).astype(jnp.float32)
    scaled = (last_state * head_gain.astype(jnp.float32)).astype(jnp.bfloat16)
    square_part = jnp.sum(last_state * last_state, axis=1)
    logit_part = jnp.dot(scaled, vocab_weight, preferred_element_type=jnp.float32)
    summed = butterfly(
        jnp.concatenate([logit_part, square_part[:, None]], axis=1), "tp", jnp.add
    )
    raw_logits, square_sum = summed[:, :-1], summed[:, -1]
    mean_square = square_sum / D
    last_norm = jnp.sqrt(mean_square)
    local_top = jnp.max(raw_logits * lax.rsqrt(mean_square + eps)[:, None], axis=1)
    top_logit = butterfly(local_top, "req", jnp.maximum)
    return (hidden, key_cache, last_norm, top_logit)


def solution(mesh):
    placed = (
        P("req", "tp"),
        P(None, "req", "tp"),
        P("req"),
        P("req", "tp"),
        P("tp", "req"),
        P("tp"),
        P("tp", "req"),
    )
    return jax.shard_map(
        local,
        mesh=mesh,
        in_specs=placed,
        out_specs=(P("req", "tp"), P("req", "tp"), P(), P()),
        check_vma=False,
    )
```

```python
import jax
import jax.numpy as jnp
from jax import lax
from jax.sharding import PartitionSpec as P

D = 7168
HD = 128
GROUP = 7
REACH = 4


theta = 5000000.0
eps = 1e-05
masked_score = -1e30


def from_behind(value, axis, steps):
    count = lax.axis_size(axis)
    initial, last = (max(0, -steps), min(count, count - steps))
    return lax.ppermute(value, axis, [(source, source + steps) for source in range(initial, last)])


def butterfly(value, axis, combine):
    count = lax.axis_size(axis)
    stride = 1
    while stride < count:
        other = lax.ppermute(value, axis, [(source, source ^ stride) for source in range(count)])
        value = combine(value, other)
        stride *= 2
    return value


def halving_scatter(value, axis):
    count = lax.axis_size(axis)
    index = lax.axis_index(axis)
    rows = value.shape[0]
    held = value.reshape(rows, count, value.shape[1] // count)
    bit = count // 2
    while bit >= 1:
        if bit < count // 2:
            held = held.astype(jnp.float32)
        half = held.shape[1] // 2
        mine = (index // bit) % 2
        keep = lax.dynamic_slice_in_dim(held, mine * half, half, 1)
        give = lax.dynamic_slice_in_dim(held, (1 - mine) * half, half, 1)
        held = keep.astype(jnp.float32) + lax.ppermute(give, axis, [(source, source ^ bit) for source in range(count)]).astype(jnp.float32)
        bit //= 2
    return held.reshape(rows, -1)


def rope_tables(positions, width):
    half_width = width // 2
    frequency = theta ** (-(jnp.arange(half_width, dtype=jnp.float32) * 2.0 / width))
    angles = positions[:, None] * frequency[None, :]
    return (jnp.cos(angles), jnp.sin(angles))


def rotate(values, cosine, sine_table):
    half_width = values.shape[-1] // 2
    first_half = values[..., :half_width]
    second_half = values[..., half_width:]
    table_shape = (cosine.shape[0],) + (1,) * (values.ndim - 2) + (half_width,)
    cosine = cosine.reshape(table_shape)
    sine_table = sine_table.reshape(table_shape)
    return jnp.concatenate(
        [
            first_half * cosine - second_half * sine_table,
            second_half * cosine + first_half * sine_table,
        ],
        axis=-1,
    )


def local(queries, key_value, segment, residual, out_weight, head_gain, vocab_weight):
    tok_rows = segment.shape[0]
    heads_kv = key_value.shape[2] // HD
    requests = lax.axis_size("req") // 2
    devices_req = lax.axis_size("req")
    device = lax.axis_index("req")
    request_ids = jnp.arange(requests, dtype=jnp.int32)

    own_kv = key_value
    width = own_kv.shape[2]
    seg_rows = -(-tok_rows // width)
    seg_flat = jnp.pad(segment, (0, seg_rows * width - tok_rows)).astype(jnp.bfloat16)
    packed = jnp.concatenate(
        [own_kv.reshape(2 * tok_rows, width), seg_flat.reshape(seg_rows, width)], axis=0
    )
    parts_kv, parts_seg = [], []
    for back in range(REACH, 0, -1):
        got = from_behind(packed, "req", back)
        parts_kv.append(got[: 2 * tok_rows].reshape(own_kv.shape))
        parts_seg.append(got[2 * tok_rows :].reshape(-1)[:tok_rows].astype(jnp.int32))
    parts_kv.append(own_kv)
    parts_seg.append(segment)
    next_first = from_behind(segment[:1], "req", -1)
    window = jnp.concatenate(parts_kv, axis=1)
    seg_window = jnp.concatenate(parts_seg, axis=0)
    span = window.shape[1]
    key_index_i = (device - REACH) * tok_rows + jnp.arange(span, dtype=jnp.int32)
    valid = key_index_i >= 0
    same = (seg_window[:, None] == seg_window[None, :]) & valid[None, :]
    start_i = jnp.min(jnp.where(same, key_index_i[None, :], jnp.int32(2**30)), axis=1)
    key_index = key_index_i.astype(jnp.float32)
    win_start = start_i.astype(jnp.float32)
    win_pos = key_index - win_start
    own_start = win_start[span - tok_rows:]
    tok_index = key_index[span - tok_rows:]
    positions = win_pos[span - tok_rows:]

    cosine, sine_table = rope_tables(win_pos, HD)
    rot_keys = rotate(
        window[0].astype(jnp.float32).reshape(span, heads_kv, HD), cosine, sine_table
    ).astype(jnp.bfloat16)
    q_cos, q_sin = cosine[span - tok_rows:], sine_table[span - tok_rows:]
    rot_query = rotate(
        queries.astype(jnp.float32).reshape(tok_rows, heads_kv, GROUP, HD), q_cos, q_sin
    ).astype(jnp.bfloat16)
    key_cache = rot_keys[span - tok_rows:].reshape(tok_rows, heads_kv * HD)
    key_rows = rot_keys
    value_rows = window[1].reshape(span, heads_kv, HD)
    q_seg = segment
    allowed = (
        (seg_window[None, :] == q_seg[:, None])
        & valid[None, :]
        & (key_index[None, :] <= tok_index[:, None])
    )
    scale = HD ** (-0.5)
    scores_part = (
        jnp.einsum("qhgd,khd->hgqk", rot_query, key_rows, preferred_element_type=jnp.float32)
        * scale
    )
    scores = jnp.where(allowed[None, None], scores_part, masked_score)
    peak = jnp.max(scores, axis=3, keepdims=True)
    weights = jnp.exp(scores - peak)
    total = jnp.sum(weights, axis=3)
    context = jnp.einsum(
        "hgqk,khd->qhgd",
        weights.astype(jnp.bfloat16),
        value_rows,
        preferred_element_type=jnp.float32,
    )
    context = context / jnp.transpose(total, (2, 0, 1))[..., None]
    attended = context.astype(jnp.bfloat16).reshape(tok_rows, heads_kv * GROUP * HD)
    following = jnp.concatenate([segment[1:], next_first])
    is_last_dev = device == devices_req - 1
    is_end = following != segment
    is_end = is_end.at[tok_rows - 1].set(is_end[tok_rows - 1] | is_last_dev)
    select = (is_end[:, None] & (segment[:, None] == request_ids[None, :])).astype(jnp.bfloat16)
    end_rows = lax.dot_general(
        select,
        jnp.concatenate([attended, residual], axis=1),
        (((0,), (0,)), ((), ())),
        preferred_element_type=jnp.float32,
    ).astype(jnp.bfloat16)
    end_rows = butterfly(end_rows, "req", jnp.add)
    attended, end_rows = lax.optimization_barrier((attended, end_rows))
    end_att, end_res = end_rows[:, : attended.shape[1]], end_rows[:, attended.shape[1] :]

    full_weight = lax.all_gather(out_weight, "req", axis=1, tiled=True)
    both = jnp.dot(
        jnp.concatenate([attended, end_att], axis=0), full_weight, preferred_element_type=jnp.float32
    ).astype(jnp.bfloat16)
    projected, end_part = both[:tok_rows], both[tok_rows:]
    end_sum = halving_scatter(end_part, "tp")
    projected, end_sum = lax.optimization_barrier((projected, end_sum))
    own_share = lax.psum_scatter(projected, "tp", scatter_dimension=1, tiled=True).astype(jnp.float32)
    hidden = (residual.astype(jnp.float32) + own_share).astype(jnp.bfloat16)
    last_state = (end_res.astype(jnp.float32) + end_sum).astype(jnp.bfloat16).astype(jnp.float32)
    scaled = (last_state * head_gain.astype(jnp.float32)).astype(jnp.bfloat16)
    square_part = jnp.sum(last_state * last_state, axis=1)
    logit_part = jnp.dot(scaled, vocab_weight, preferred_element_type=jnp.float32)
    summed = butterfly(
        jnp.concatenate([logit_part, square_part[:, None]], axis=1), "tp", jnp.add
    )
    raw_logits, square_sum = summed[:, :-1], summed[:, -1]
    mean_square = square_sum / D
    last_norm = jnp.sqrt(mean_square)
    local_top = jnp.max(raw_logits * lax.rsqrt(mean_square + eps)[:, None], axis=1)
    top_logit = butterfly(local_top, "req", jnp.maximum)
    return (hidden, key_cache, last_norm, top_logit)


def solution(mesh):
    placed = (
        P("req", "tp"),
        P(None, "req", "tp"),
        P("req"),
        P("req", "tp"),
        P("tp", "req"),
        P("tp"),
        P("tp", "req"),
    )
    return jax.shard_map(
        local,
        mesh=mesh,
        in_specs=placed,
        out_specs=(P("req", "tp"), P("req", "tp"), P(), P()),
        check_vma=False,
    )
```

```python
import jax
import jax.numpy as jnp
from jax import lax
from jax.sharding import PartitionSpec as P

D = 7168
HD = 128
GROUP = 7
REACH = 4


theta = 5000000.0
eps = 1e-05
masked_score = -1e30


def from_behind(value, axis, steps):
    count = lax.axis_size(axis)
    initial, last = (max(0, -steps), min(count, count - steps))
    return lax.ppermute(value, axis, [(source, source + steps) for source in range(initial, last)])


def butterfly(value, axis, combine):
    count = lax.axis_size(axis)
    stride = 1
    while stride < count:
        other = lax.ppermute(value, axis, [(source, source ^ stride) for source in range(count)])
        value = combine(value, other)
        stride *= 2
    return value


def halving_scatter(value, axis):
    count = lax.axis_size(axis)
    index = lax.axis_index(axis)
    rows = value.shape[0]
    held = value.reshape(rows, count, value.shape[1] // count)
    bit = count // 2
    while bit >= 1:
        if bit < count // 2:
            held = held.astype(jnp.float32)
        half = held.shape[1] // 2
        mine = (index // bit) % 2
        keep = lax.dynamic_slice_in_dim(held, mine * half, half, 1)
        give = lax.dynamic_slice_in_dim(held, (1 - mine) * half, half, 1)
        held = keep.astype(jnp.float32) + lax.ppermute(give, axis, [(source, source ^ bit) for source in range(count)]).astype(jnp.float32)
        bit //= 2
    return held.reshape(rows, -1)


def rope_tables(positions, width):
    half_width = width // 2
    frequency = theta ** (-(jnp.arange(half_width, dtype=jnp.float32) * 2.0 / width))
    angles = positions[:, None] * frequency[None, :]
    return (jnp.cos(angles), jnp.sin(angles))


def rotate(values, cosine, sine_table):
    half_width = values.shape[-1] // 2
    first_half = values[..., :half_width]
    second_half = values[..., half_width:]
    table_shape = (cosine.shape[0],) + (1,) * (values.ndim - 2) + (half_width,)
    cosine = cosine.reshape(table_shape)
    sine_table = sine_table.reshape(table_shape)
    return jnp.concatenate(
        [
            first_half * cosine - second_half * sine_table,
            second_half * cosine + first_half * sine_table,
        ],
        axis=-1,
    )


def local(queries, key_value, segment, residual, out_weight, head_gain, vocab_weight):
    tok_rows = segment.shape[0]
    heads_kv = key_value.shape[2] // HD
    requests = lax.axis_size("req") // 2
    devices_req = lax.axis_size("req")
    device = lax.axis_index("req")
    request_ids = jnp.arange(requests, dtype=jnp.int32)

    own_kv = key_value
    width = own_kv.shape[2]
    seg_rows = -(-tok_rows // width)
    seg_flat = jnp.pad(segment, (0, seg_rows * width - tok_rows)).astype(jnp.bfloat16)
    packed = jnp.concatenate(
        [own_kv.reshape(2 * tok_rows, width), seg_flat.reshape(seg_rows, width)], axis=0
    )
    parts_kv, parts_seg = [], []
    for back in range(REACH, 0, -1):
        got = from_behind(packed, "req", back)
        parts_kv.append(got[: 2 * tok_rows].reshape(own_kv.shape))
        parts_seg.append(got[2 * tok_rows :].reshape(-1)[:tok_rows].astype(jnp.int32))
    parts_kv.append(own_kv)
    parts_seg.append(segment)
    next_first = from_behind(segment[:1], "req", -1)
    window = jnp.concatenate(parts_kv, axis=1)
    seg_window = jnp.concatenate(parts_seg, axis=0)
    span = window.shape[1]
    key_index_i = (device - REACH) * tok_rows + jnp.arange(span, dtype=jnp.int32)
    valid = key_index_i >= 0
    same = (seg_window[:, None] == seg_window[None, :]) & valid[None, :]
    start_i = jnp.min(jnp.where(same, key_index_i[None, :], jnp.int32(2**30)), axis=1)
    key_index = key_index_i.astype(jnp.float32)
    win_start = start_i.astype(jnp.float32)
    win_pos = key_index - win_start
    own_start = win_start[span - tok_rows:]
    tok_index = key_index[span - tok_rows:]
    positions = win_pos[span - tok_rows:]

    cosine, sine_table = rope_tables(win_pos, HD)
    rot_keys = rotate(
        window[0].astype(jnp.float32).reshape(span, heads_kv, HD), cosine, sine_table
    ).astype(jnp.bfloat16)
    q_cos, q_sin = cosine[span - tok_rows:], sine_table[span - tok_rows:]
    rot_query = rotate(
        queries.astype(jnp.float32).reshape(tok_rows, heads_kv, GROUP, HD), q_cos, q_sin
    ).astype(jnp.bfloat16)
    key_cache = rot_keys[span - tok_rows:].reshape(tok_rows, heads_kv * HD)
    key_rows = rot_keys
    value_rows = window[1].reshape(span, heads_kv, HD)
    q_seg = segment
    allowed = (
        (seg_window[None, :] == q_seg[:, None])
        & valid[None, :]
        & (key_index[None, :] <= tok_index[:, None])
    )
    scale = HD ** (-0.5)
    scores_part = (
        jnp.einsum("qhgd,khd->hgqk", rot_query, key_rows, preferred_element_type=jnp.float32)
        * scale
    )
    scores = jnp.where(allowed[None, None], scores_part, masked_score)
    peak = jnp.max(scores, axis=3, keepdims=True)
    weights = jnp.exp(scores - peak)
    total = jnp.sum(weights, axis=3)
    context = jnp.einsum(
        "hgqk,khd->qhgd",
        weights.astype(jnp.bfloat16),
        value_rows,
        preferred_element_type=jnp.float32,
    )
    context = context / jnp.transpose(total, (2, 0, 1))[..., None]
    attended = context.astype(jnp.bfloat16).reshape(tok_rows, heads_kv * GROUP * HD)
    following = jnp.concatenate([segment[1:], next_first])
    is_last_dev = device == devices_req - 1
    is_end = following != segment
    is_end = is_end.at[tok_rows - 1].set(is_end[tok_rows - 1] | is_last_dev)
    select = (is_end[:, None] & (segment[:, None] == request_ids[None, :])).astype(jnp.bfloat16)
    end_rows = lax.dot_general(
        select,
        jnp.concatenate([attended, residual], axis=1),
        (((0,), (0,)), ((), ())),
        preferred_element_type=jnp.float32,
    ).astype(jnp.bfloat16)
    end_rows = butterfly(end_rows, "req", jnp.add)
    attended, end_rows = lax.optimization_barrier((attended, end_rows))
    end_att, end_res = end_rows[:, : attended.shape[1]], end_rows[:, attended.shape[1] :]

    full_weight = lax.all_gather(out_weight, "req", axis=1, tiled=True)
    both = jnp.dot(
        jnp.concatenate([attended, end_att], axis=0), full_weight, preferred_element_type=jnp.float32
    ).astype(jnp.bfloat16)
    projected, end_part = both[:tok_rows], both[tok_rows:]
    end_sum = lax.psum_scatter(end_part, "tp", scatter_dimension=1, tiled=True).astype(jnp.float32)
    projected, end_sum = lax.optimization_barrier((projected, end_sum))
    own_share = lax.psum_scatter(projected, "tp", scatter_dimension=1, tiled=True).astype(jnp.float32)
    hidden = (residual.astype(jnp.float32) + own_share).astype(jnp.bfloat16)
    last_state = (end_res.astype(jnp.float32) + end_sum).astype(jnp.bfloat16).astype(jnp.float32)
    scaled = (last_state * head_gain.astype(jnp.float32)).astype(jnp.bfloat16)
    square_part = jnp.sum(last_state * last_state, axis=1)
    logit_part = jnp.dot(scaled, vocab_weight, preferred_element_type=jnp.float32)
    summed = butterfly(
        jnp.concatenate([logit_part, square_part[:, None]], axis=1), "tp", jnp.add
    )
    raw_logits, square_sum = summed[:, :-1], summed[:, -1]
    mean_square = square_sum / D
    last_norm = jnp.sqrt(mean_square)
    local_top = jnp.max(raw_logits * lax.rsqrt(mean_square + eps)[:, None], axis=1)
    top_logit = butterfly(local_top, "req", jnp.maximum)
    return (hidden, key_cache, last_norm, top_logit)


def solution(mesh):
    placed = (
        P("req", "tp"),
        P(None, "req", "tp"),
        P("req"),
        P("req", "tp"),
        P("tp", "req"),
        P("tp"),
        P("tp", "req"),
    )
    return jax.shard_map(
        local,
        mesh=mesh,
        in_specs=placed,
        out_specs=(P("req", "tp"), P("req", "tp"), P(), P()),
        check_vma=False,
    )
```

```python
import jax
import jax.numpy as jnp
from jax import lax
from jax.sharding import PartitionSpec as P

D = 7168
HD = 128
GROUP = 7
REACH = 4


theta = 5000000.0
eps = 1e-05
masked_score = -1e30


def from_behind(value, axis, steps):
    count = lax.axis_size(axis)
    initial, last = (max(0, -steps), min(count, count - steps))
    return lax.ppermute(value, axis, [(source, source + steps) for source in range(initial, last)])


def butterfly(value, axis, combine):
    count = lax.axis_size(axis)
    stride = 1
    while stride < count:
        other = lax.ppermute(value, axis, [(source, source ^ stride) for source in range(count)])
        value = combine(value, other)
        stride *= 2
    return value


def halving_scatter(value, axis):
    count = lax.axis_size(axis)
    index = lax.axis_index(axis)
    rows, width = value.shape[0], value.shape[1] // count
    held = value.reshape(rows, count, width)
    bit = 1
    while bit < count:
        mine = (index // bit) % 2
        pairs = held.reshape(rows, held.shape[1] // 2, 2, width)
        keep = lax.dynamic_index_in_dim(pairs, mine, 2, keepdims=False)
        give = lax.dynamic_index_in_dim(pairs, 1 - mine, 2, keepdims=False)
        moved = lax.ppermute(give, axis, [(source, source ^ bit) for source in range(count)])
        held = (keep.astype(jnp.float32) + moved.astype(jnp.float32)).astype(value.dtype)
        bit *= 2
    return held.reshape(rows, width).astype(jnp.float32)


def rope_tables(positions, width):
    half_width = width // 2
    frequency = theta ** (-(jnp.arange(half_width, dtype=jnp.float32) * 2.0 / width))
    angles = positions[:, None] * frequency[None, :]
    return (jnp.cos(angles), jnp.sin(angles))


def rotate(values, cosine, sine_table):
    half_width = values.shape[-1] // 2
    first_half = values[..., :half_width]
    second_half = values[..., half_width:]
    table_shape = (cosine.shape[0],) + (1,) * (values.ndim - 2) + (half_width,)
    cosine = cosine.reshape(table_shape)
    sine_table = sine_table.reshape(table_shape)
    return jnp.concatenate(
        [
            first_half * cosine - second_half * sine_table,
            second_half * cosine + first_half * sine_table,
        ],
        axis=-1,
    )


def local(queries, key_value, segment, residual, out_weight, head_gain, vocab_weight):
    tok_rows = segment.shape[0]
    heads_kv = key_value.shape[2] // HD
    requests = lax.axis_size("req") // 2
    devices_req = lax.axis_size("req")
    device = lax.axis_index("req")
    request_ids = jnp.arange(requests, dtype=jnp.int32)

    own_kv = key_value
    width = own_kv.shape[2]
    seg_rows = -(-tok_rows // width)
    seg_flat = jnp.pad(segment, (0, seg_rows * width - tok_rows)).astype(jnp.bfloat16)
    packed = jnp.concatenate(
        [own_kv.reshape(2 * tok_rows, width), seg_flat.reshape(seg_rows, width)], axis=0
    )
    parts_kv, parts_seg = [], []
    for back in range(REACH, 0, -1):
        got = from_behind(packed, "req", back)
        parts_kv.append(got[: 2 * tok_rows].reshape(own_kv.shape))
        parts_seg.append(got[2 * tok_rows :].reshape(-1)[:tok_rows].astype(jnp.int32))
    parts_kv.append(own_kv)
    parts_seg.append(segment)
    next_first = from_behind(segment[:1], "req", -1)
    window = jnp.concatenate(parts_kv, axis=1)
    seg_window = jnp.concatenate(parts_seg, axis=0)
    span = window.shape[1]
    key_index_i = (device - REACH) * tok_rows + jnp.arange(span, dtype=jnp.int32)
    valid = key_index_i >= 0
    same = (seg_window[:, None] == seg_window[None, :]) & valid[None, :]
    start_i = jnp.min(jnp.where(same, key_index_i[None, :], jnp.int32(2**30)), axis=1)
    key_index = key_index_i.astype(jnp.float32)
    win_start = start_i.astype(jnp.float32)
    win_pos = key_index - win_start
    own_start = win_start[span - tok_rows:]
    tok_index = key_index[span - tok_rows:]
    positions = win_pos[span - tok_rows:]

    cosine, sine_table = rope_tables(win_pos, HD)
    rot_keys = rotate(
        window[0].astype(jnp.float32).reshape(span, heads_kv, HD), cosine, sine_table
    ).astype(jnp.bfloat16)
    q_cos, q_sin = cosine[span - tok_rows:], sine_table[span - tok_rows:]
    rot_query = rotate(
        queries.astype(jnp.float32).reshape(tok_rows, heads_kv, GROUP, HD), q_cos, q_sin
    ).astype(jnp.bfloat16)
    key_cache = rot_keys[span - tok_rows:].reshape(tok_rows, heads_kv * HD)
    key_rows = rot_keys
    value_rows = window[1].reshape(span, heads_kv, HD)
    q_seg = segment
    allowed = (
        (seg_window[None, :] == q_seg[:, None])
        & valid[None, :]
        & (key_index[None, :] <= tok_index[:, None])
    )
    scale = HD ** (-0.5)
    scores_part = (
        jnp.einsum("qhgd,khd->hgqk", rot_query, key_rows, preferred_element_type=jnp.float32)
        * scale
    )
    scores = jnp.where(allowed[None, None], scores_part, masked_score)
    peak = jnp.max(scores, axis=3, keepdims=True)
    weights = jnp.exp(scores - peak)
    total = jnp.sum(weights, axis=3)
    context = jnp.einsum(
        "hgqk,khd->qhgd",
        weights.astype(jnp.bfloat16),
        value_rows,
        preferred_element_type=jnp.float32,
    )
    context = context / jnp.transpose(total, (2, 0, 1))[..., None]
    attended = context.astype(jnp.bfloat16).reshape(tok_rows, heads_kv * GROUP * HD)
    following = jnp.concatenate([segment[1:], next_first])
    is_last_dev = device == devices_req - 1
    is_end = following != segment
    is_end = is_end.at[tok_rows - 1].set(is_end[tok_rows - 1] | is_last_dev)
    select = (is_end[:, None] & (segment[:, None] == request_ids[None, :])).astype(jnp.bfloat16)
    end_rows = lax.dot_general(
        select,
        jnp.concatenate([attended, residual], axis=1),
        (((0,), (0,)), ((), ())),
        preferred_element_type=jnp.float32,
    ).astype(jnp.bfloat16)
    end_rows = butterfly(end_rows, "req", jnp.add)
    attended, end_rows = lax.optimization_barrier((attended, end_rows))
    end_att, end_res = end_rows[:, : attended.shape[1]], end_rows[:, attended.shape[1] :]

    full_weight = lax.all_gather(out_weight, "req", axis=1, tiled=True)
    both = jnp.dot(
        jnp.concatenate([attended, end_att], axis=0), full_weight, preferred_element_type=jnp.float32
    ).astype(jnp.bfloat16)
    projected, end_part = both[:tok_rows], both[tok_rows:]
    end_sum = halving_scatter(end_part, "tp")
    projected, end_sum = lax.optimization_barrier((projected, end_sum))
    own_share = lax.psum_scatter(projected, "tp", scatter_dimension=1, tiled=True).astype(jnp.float32)
    hidden = (residual.astype(jnp.float32) + own_share).astype(jnp.bfloat16)
    last_state = (end_res.astype(jnp.float32) + end_sum).astype(jnp.bfloat16).astype(jnp.float32)
    scaled = (last_state * head_gain.astype(jnp.float32)).astype(jnp.bfloat16)
    square_part = jnp.sum(last_state * last_state, axis=1)
    logit_part = jnp.dot(scaled, vocab_weight, preferred_element_type=jnp.float32)
    summed = butterfly(
        jnp.concatenate([logit_part, square_part[:, None]], axis=1), "tp", jnp.add
    )
    raw_logits, square_sum = summed[:, :-1], summed[:, -1]
    mean_square = square_sum / D
    last_norm = jnp.sqrt(mean_square)
    local_top = jnp.max(raw_logits * lax.rsqrt(mean_square + eps)[:, None], axis=1)
    top_logit = butterfly(local_top, "req", jnp.maximum)
    return (hidden, key_cache, last_norm, top_logit)


def solution(mesh):
    placed = (
        P("req", "tp"),
        P(None, "req", "tp"),
        P("req"),
        P("req", "tp"),
        P("tp", "req"),
        P("tp"),
        P("tp", "req"),
    )
    return jax.shard_map(
        local,
        mesh=mesh,
        in_specs=placed,
        out_specs=(P("req", "tp"), P("req", "tp"), P(), P()),
        check_vma=False,
    )
```

```python
import jax
import jax.numpy as jnp
from jax import lax
from jax.sharding import PartitionSpec as P

D = 7168
HD = 128
GROUP = 7
REACH = 4


theta = 5000000.0
eps = 1e-05
masked_score = -1e30


def from_behind(value, axis, steps):
    count = lax.axis_size(axis)
    initial, last = (max(0, -steps), min(count, count - steps))
    return lax.ppermute(value, axis, [(source, source + steps) for source in range(initial, last)])


def butterfly(value, axis, combine):
    count = lax.axis_size(axis)
    stride = 1
    while stride < count:
        other = lax.ppermute(value, axis, [(source, source ^ stride) for source in range(count)])
        value = combine(value, other)
        stride *= 2
    return value


def halving_scatter(value, axis):
    count = lax.axis_size(axis)
    index = lax.axis_index(axis)
    rows, width = value.shape[1], value.shape[2]
    held = jnp.moveaxis(value, 0, 1)
    bit = 1
    while bit < count:
        mine = (index // bit) % 2
        pairs = held.reshape(rows, held.shape[1] // 2, 2, width)
        keep = lax.dynamic_index_in_dim(pairs, mine, 2, keepdims=False)
        give = lax.dynamic_index_in_dim(pairs, 1 - mine, 2, keepdims=False)
        moved = lax.ppermute(give, axis, [(source, source ^ bit) for source in range(count)])
        held = (keep.astype(jnp.float32) + moved.astype(jnp.float32)).astype(value.dtype)
        bit *= 2
    return held.reshape(rows, width).astype(jnp.float32)


def rope_tables(positions, width):
    half_width = width // 2
    frequency = theta ** (-(jnp.arange(half_width, dtype=jnp.float32) * 2.0 / width))
    angles = positions[:, None] * frequency[None, :]
    return (jnp.cos(angles), jnp.sin(angles))


def rotate(values, cosine, sine_table):
    half_width = values.shape[-1] // 2
    first_half = values[..., :half_width]
    second_half = values[..., half_width:]
    table_shape = (cosine.shape[0],) + (1,) * (values.ndim - 2) + (half_width,)
    cosine = cosine.reshape(table_shape)
    sine_table = sine_table.reshape(table_shape)
    return jnp.concatenate(
        [
            first_half * cosine - second_half * sine_table,
            second_half * cosine + first_half * sine_table,
        ],
        axis=-1,
    )


def local(queries, key_value, segment, residual, out_weight, head_gain, vocab_weight):
    tok_rows = segment.shape[0]
    heads_kv = key_value.shape[2] // HD
    requests = lax.axis_size("req") // 2
    devices_req = lax.axis_size("req")
    device = lax.axis_index("req")
    request_ids = jnp.arange(requests, dtype=jnp.int32)

    own_kv = key_value
    width = own_kv.shape[2]
    seg_rows = -(-tok_rows // width)
    seg_flat = jnp.pad(segment, (0, seg_rows * width - tok_rows)).astype(jnp.bfloat16)
    packed = jnp.concatenate(
        [own_kv.reshape(2 * tok_rows, width), seg_flat.reshape(seg_rows, width)], axis=0
    )
    parts_kv, parts_seg = [], []
    for back in range(REACH, 0, -1):
        got = from_behind(packed, "req", back)
        parts_kv.append(got[: 2 * tok_rows].reshape(own_kv.shape))
        parts_seg.append(got[2 * tok_rows :].reshape(-1)[:tok_rows].astype(jnp.int32))
    parts_kv.append(own_kv)
    parts_seg.append(segment)
    next_first = from_behind(segment[:1], "req", -1)
    window = jnp.concatenate(parts_kv, axis=1)
    seg_window = jnp.concatenate(parts_seg, axis=0)
    span = window.shape[1]
    key_index_i = (device - REACH) * tok_rows + jnp.arange(span, dtype=jnp.int32)
    valid = key_index_i >= 0
    same = (seg_window[:, None] == seg_window[None, :]) & valid[None, :]
    start_i = jnp.min(jnp.where(same, key_index_i[None, :], jnp.int32(2**30)), axis=1)
    key_index = key_index_i.astype(jnp.float32)
    win_start = start_i.astype(jnp.float32)
    win_pos = key_index - win_start
    own_start = win_start[span - tok_rows:]
    tok_index = key_index[span - tok_rows:]
    positions = win_pos[span - tok_rows:]

    cosine, sine_table = rope_tables(win_pos, HD)
    rot_keys = rotate(
        window[0].astype(jnp.float32).reshape(span, heads_kv, HD), cosine, sine_table
    ).astype(jnp.bfloat16)
    q_cos, q_sin = cosine[span - tok_rows:], sine_table[span - tok_rows:]
    rot_query = rotate(
        queries.astype(jnp.float32).reshape(tok_rows, heads_kv, GROUP, HD), q_cos, q_sin
    ).astype(jnp.bfloat16)
    key_cache = rot_keys[span - tok_rows:].reshape(tok_rows, heads_kv * HD)
    key_rows = rot_keys
    value_rows = window[1].reshape(span, heads_kv, HD)
    q_seg = segment
    allowed = (
        (seg_window[None, :] == q_seg[:, None])
        & valid[None, :]
        & (key_index[None, :] <= tok_index[:, None])
    )
    scale = HD ** (-0.5)
    scores_part = (
        jnp.einsum("qhgd,khd->hgqk", rot_query, key_rows, preferred_element_type=jnp.float32)
        * scale
    )
    scores = jnp.where(allowed[None, None], scores_part, masked_score)
    peak = jnp.max(scores, axis=3, keepdims=True)
    weights = jnp.exp(scores - peak)
    total = jnp.sum(weights, axis=3)
    context = jnp.einsum(
        "hgqk,khd->qhgd",
        weights.astype(jnp.bfloat16),
        value_rows,
        preferred_element_type=jnp.float32,
    )
    context = context / jnp.transpose(total, (2, 0, 1))[..., None]
    attended = context.astype(jnp.bfloat16).reshape(tok_rows, heads_kv * GROUP * HD)
    following = jnp.concatenate([segment[1:], next_first])
    is_last_dev = device == devices_req - 1
    is_end = following != segment
    is_end = is_end.at[tok_rows - 1].set(is_end[tok_rows - 1] | is_last_dev)
    select = (is_end[:, None] & (segment[:, None] == request_ids[None, :])).astype(jnp.bfloat16)
    end_rows = lax.dot_general(
        select,
        jnp.concatenate([attended, residual], axis=1),
        (((0,), (0,)), ((), ())),
        preferred_element_type=jnp.float32,
    ).astype(jnp.bfloat16)
    end_rows = butterfly(end_rows, "req", jnp.add)
    attended, end_rows = lax.optimization_barrier((attended, end_rows))
    end_att, end_res = end_rows[:, : attended.shape[1]], end_rows[:, attended.shape[1] :]

    full_weight = lax.all_gather(out_weight, "req", axis=1, tiled=True)
    groups = lax.axis_size("tp")
    both = jnp.einsum(
        "tk,kgn->gtn",
        jnp.concatenate([attended, end_att], axis=0),
        full_weight.reshape(full_weight.shape[0], groups, -1),
        preferred_element_type=jnp.float32,
    ).astype(jnp.bfloat16)
    projected, end_part = both[:, :tok_rows], both[:, tok_rows:]
    end_sum = halving_scatter(end_part, "tp")
    projected, end_sum = lax.optimization_barrier((projected, end_sum))
    own_share = lax.psum_scatter(projected, "tp", scatter_dimension=0, tiled=True)[0].astype(jnp.float32)
    hidden = (residual.astype(jnp.float32) + own_share).astype(jnp.bfloat16)
    last_state = (end_res.astype(jnp.float32) + end_sum).astype(jnp.bfloat16).astype(jnp.float32)
    scaled = (last_state * head_gain.astype(jnp.float32)).astype(jnp.bfloat16)
    square_part = jnp.sum(last_state * last_state, axis=1)
    logit_part = jnp.dot(scaled, vocab_weight, preferred_element_type=jnp.float32)
    summed = butterfly(
        jnp.concatenate([logit_part, square_part[:, None]], axis=1), "tp", jnp.add
    )
    raw_logits, square_sum = summed[:, :-1], summed[:, -1]
    mean_square = square_sum / D
    last_norm = jnp.sqrt(mean_square)
    local_top = jnp.max(raw_logits * lax.rsqrt(mean_square + eps)[:, None], axis=1)
    top_logit = butterfly(local_top, "req", jnp.maximum)
    return (hidden, key_cache, last_norm, top_logit)


def solution(mesh):
    placed = (
        P("req", "tp"),
        P(None, "req", "tp"),
        P("req"),
        P("req", "tp"),
        P("tp", "req"),
        P("tp"),
        P("tp", "req"),
    )
    return jax.shard_map(
        local,
        mesh=mesh,
        in_specs=placed,
        out_specs=(P("req", "tp"), P("req", "tp"), P(), P()),
        check_vma=False,
    )
```

```python
import jax
import jax.numpy as jnp
from jax import lax
from jax.sharding import PartitionSpec as P

D = 7168
HD = 128
GROUP = 7
REACH = 4


theta = 5000000.0
eps = 1e-05
masked_score = -1e30


def from_behind(value, axis, steps):
    count = lax.axis_size(axis)
    initial, last = (max(0, -steps), min(count, count - steps))
    return lax.ppermute(value, axis, [(source, source + steps) for source in range(initial, last)])


def butterfly(value, axis, combine):
    count = lax.axis_size(axis)
    stride = 1
    while stride < count:
        other = lax.ppermute(value, axis, [(source, source ^ stride) for source in range(count)])
        value = combine(value, other)
        stride *= 2
    return value


def halving_scatter(value, axis):
    count = lax.axis_size(axis)
    index = lax.axis_index(axis)
    rows, width = value.shape[1], value.shape[2]
    held = jnp.moveaxis(value, 0, 1)
    bit = 1
    while bit < count:
        mine = (index // bit) % 2
        pairs = held.reshape(rows, held.shape[1] // 2, 2, width)
        keep = lax.dynamic_index_in_dim(pairs, mine, 2, keepdims=False)
        give = lax.dynamic_index_in_dim(pairs, 1 - mine, 2, keepdims=False)
        moved = lax.ppermute(give, axis, [(source, source ^ bit) for source in range(count)])
        held = (keep.astype(jnp.float32) + moved.astype(jnp.float32)).astype(value.dtype)
        bit *= 2
    return held.reshape(rows, width).astype(jnp.float32)


def rope_tables(positions, width):
    half_width = width // 2
    frequency = theta ** (-(jnp.arange(half_width, dtype=jnp.float32) * 2.0 / width))
    angles = positions[:, None] * frequency[None, :]
    return (jnp.cos(angles), jnp.sin(angles))


def rotate(values, cosine, sine_table):
    half_width = values.shape[-1] // 2
    first_half = values[..., :half_width]
    second_half = values[..., half_width:]
    table_shape = (cosine.shape[0],) + (1,) * (values.ndim - 2) + (half_width,)
    cosine = cosine.reshape(table_shape)
    sine_table = sine_table.reshape(table_shape)
    return jnp.concatenate(
        [
            first_half * cosine - second_half * sine_table,
            second_half * cosine + first_half * sine_table,
        ],
        axis=-1,
    )


def local(queries, key_value, segment, residual, out_weight, head_gain, vocab_weight):
    tok_rows = segment.shape[0]
    heads_kv = key_value.shape[2] // HD
    requests = lax.axis_size("req") // 2
    devices_req = lax.axis_size("req")
    device = lax.axis_index("req")
    request_ids = jnp.arange(requests, dtype=jnp.int32)

    own_kv = key_value
    width = own_kv.shape[2]
    seg_rows = -(-tok_rows // width)
    seg_flat = jnp.pad(segment, (0, seg_rows * width - tok_rows)).astype(jnp.bfloat16)
    packed = jnp.concatenate(
        [own_kv.reshape(2 * tok_rows, width), seg_flat.reshape(seg_rows, width)], axis=0
    )
    parts_kv, parts_seg = [], []
    for back in range(REACH, 0, -1):
        got = from_behind(packed, "req", back)
        parts_kv.append(got[: 2 * tok_rows].reshape(own_kv.shape))
        parts_seg.append(got[2 * tok_rows :].reshape(-1)[:tok_rows].astype(jnp.int32))
    parts_kv.append(own_kv)
    parts_seg.append(segment)
    next_first = from_behind(segment[:1], "req", -1)
    window = jnp.concatenate(parts_kv, axis=1)
    seg_window = jnp.concatenate(parts_seg, axis=0)
    span = window.shape[1]
    key_index_i = (device - REACH) * tok_rows + jnp.arange(span, dtype=jnp.int32)
    valid = key_index_i >= 0
    same = (seg_window[:, None] == seg_window[None, :]) & valid[None, :]
    start_i = jnp.min(jnp.where(same, key_index_i[None, :], jnp.int32(2**30)), axis=1)
    key_index = key_index_i.astype(jnp.float32)
    win_start = start_i.astype(jnp.float32)
    win_pos = key_index - win_start
    own_start = win_start[span - tok_rows:]
    tok_index = key_index[span - tok_rows:]
    positions = win_pos[span - tok_rows:]

    cosine, sine_table = rope_tables(win_pos, HD)
    rot_keys = rotate(
        window[0].astype(jnp.float32).reshape(span, heads_kv, HD), cosine, sine_table
    ).astype(jnp.bfloat16)
    q_cos, q_sin = cosine[span - tok_rows:], sine_table[span - tok_rows:]
    rot_query = rotate(
        queries.astype(jnp.float32).reshape(tok_rows, heads_kv, GROUP, HD), q_cos, q_sin
    ).astype(jnp.bfloat16)
    key_cache = rot_keys[span - tok_rows:].reshape(tok_rows, heads_kv * HD)
    key_rows = rot_keys
    value_rows = window[1].reshape(span, heads_kv, HD)
    q_seg = segment
    allowed = (
        (seg_window[None, :] == q_seg[:, None])
        & valid[None, :]
        & (key_index[None, :] <= tok_index[:, None])
    )
    scale = HD ** (-0.5)
    scores_part = (
        jnp.einsum("qhgd,khd->hgqk", rot_query, key_rows, preferred_element_type=jnp.float32)
        * scale
    )
    scores = jnp.where(allowed[None, None], scores_part, masked_score)
    peak = jnp.max(scores, axis=3, keepdims=True)
    weights = jnp.exp(scores - peak)
    total = jnp.sum(weights, axis=3)
    context = jnp.einsum(
        "hgqk,khd->qhgd",
        weights.astype(jnp.bfloat16),
        value_rows,
        preferred_element_type=jnp.float32,
    )
    context = context / jnp.transpose(total, (2, 0, 1))[..., None]
    attended = context.astype(jnp.bfloat16).reshape(tok_rows, heads_kv * GROUP * HD)
    following = jnp.concatenate([segment[1:], next_first])
    is_last_dev = device == devices_req - 1
    is_end = following != segment
    is_end = is_end.at[tok_rows - 1].set(is_end[tok_rows - 1] | is_last_dev)
    select = (is_end[:, None] & (segment[:, None] == request_ids[None, :])).astype(jnp.bfloat16)
    end_rows = lax.dot_general(
        select,
        jnp.concatenate([attended, residual], axis=1),
        (((0,), (0,)), ((), ())),
        preferred_element_type=jnp.float32,
    ).astype(jnp.bfloat16)
    end_rows = butterfly(end_rows, "req", jnp.add)
    attended, end_rows = lax.optimization_barrier((attended, end_rows))
    end_att, end_res = end_rows[:, : attended.shape[1]], end_rows[:, attended.shape[1] :]

    full_weight = lax.all_gather(out_weight, "req", axis=1, tiled=True)
    groups = lax.axis_size("tp")
    both = jnp.einsum(
        "tk,kgn->gtn",
        jnp.concatenate([attended, end_att], axis=0),
        full_weight.reshape(full_weight.shape[0], groups, -1),
        preferred_element_type=jnp.float32,
    ).astype(jnp.bfloat16)
    end_part = both[:, tok_rows:]
    end_sum = halving_scatter(end_part, "tp")
    both, end_sum = lax.optimization_barrier((both, end_sum))
    own_share = lax.psum_scatter(both, "tp", scatter_dimension=0, tiled=True)[0, :tok_rows]
    own_share = own_share.astype(jnp.float32)
    hidden = (residual.astype(jnp.float32) + own_share).astype(jnp.bfloat16)
    last_state = (end_res.astype(jnp.float32) + end_sum).astype(jnp.bfloat16).astype(jnp.float32)
    scaled = (last_state * head_gain.astype(jnp.float32)).astype(jnp.bfloat16)
    square_part = jnp.sum(last_state * last_state, axis=1)
    logit_part = jnp.dot(scaled, vocab_weight, preferred_element_type=jnp.float32)
    summed = butterfly(
        jnp.concatenate([logit_part, square_part[:, None]], axis=1).astype(jnp.bfloat16), "tp", jnp.add
    ).astype(jnp.float32)
    raw_logits, square_sum = summed[:, :-1], summed[:, -1]
    mean_square = square_sum / D
    last_norm = jnp.sqrt(mean_square)
    local_top = jnp.max(raw_logits * lax.rsqrt(mean_square + eps)[:, None], axis=1)
    top_logit = butterfly(local_top, "req", jnp.maximum)
    return (hidden, key_cache, last_norm, top_logit)


def solution(mesh):
    placed = (
        P("req", "tp"),
        P(None, "req", "tp"),
        P("req"),
        P("req", "tp"),
        P("tp", "req"),
        P("tp"),
        P("tp", "req"),
    )
    return jax.shard_map(
        local,
        mesh=mesh,
        in_specs=placed,
        out_specs=(P("req", "tp"), P("req", "tp"), P(), P()),
        check_vma=False,
    )
```

```python
import jax
import jax.numpy as jnp
from jax import lax
from jax.sharding import Mesh, PartitionSpec as P

D = 7168
HD = 128
GROUP = 7
REACH = 4
REQ = ("z", "x", "c")


theta = 5000000.0
eps = 1e-05
masked_score = -1e30


def from_behind(value, axis, steps):
    count = lax.axis_size(axis)
    initial, last = (max(0, -steps), min(count, count - steps))
    return lax.ppermute(value, axis, [(source, source + steps) for source in range(initial, last)])


def butterfly(value, axis, combine):
    count = lax.axis_size(axis)
    stride = 1
    while stride < count:
        other = lax.ppermute(value, axis, [(source, source ^ stride) for source in range(count)])
        value = combine(value, other)
        stride *= 2
    return value


def halving_scatter(value, axis):
    count = lax.axis_size(axis)
    index = lax.axis_index(axis)
    rows, width = value.shape[1], value.shape[2]
    held = jnp.moveaxis(value, 0, 1)
    bit = 1
    while bit < count:
        mine = (index // bit) % 2
        pairs = held.reshape(rows, held.shape[1] // 2, 2, width)
        keep = lax.dynamic_index_in_dim(pairs, mine, 2, keepdims=False)
        give = lax.dynamic_index_in_dim(pairs, 1 - mine, 2, keepdims=False)
        moved = lax.ppermute(give, axis, [(source, source ^ bit) for source in range(count)])
        held = (keep.astype(jnp.float32) + moved.astype(jnp.float32)).astype(value.dtype)
        bit *= 2
    return held.reshape(rows, width).astype(jnp.float32)


def rope_tables(positions, width):
    half_width = width // 2
    frequency = theta ** (-(jnp.arange(half_width, dtype=jnp.float32) * 2.0 / width))
    angles = positions[:, None] * frequency[None, :]
    return (jnp.cos(angles), jnp.sin(angles))


def rotate(values, cosine, sine_table):
    half_width = values.shape[-1] // 2
    first_half = values[..., :half_width]
    second_half = values[..., half_width:]
    table_shape = (cosine.shape[0],) + (1,) * (values.ndim - 2) + (half_width,)
    cosine = cosine.reshape(table_shape)
    sine_table = sine_table.reshape(table_shape)
    return jnp.concatenate(
        [
            first_half * cosine - second_half * sine_table,
            second_half * cosine + first_half * sine_table,
        ],
        axis=-1,
    )


def local(queries, key_value, segment, residual, out_weight, head_gain, vocab_weight):
    tok_rows = segment.shape[0]
    heads_kv = key_value.shape[2] // HD
    requests = lax.axis_size(REQ) // 2
    devices_req = lax.axis_size(REQ)
    device = lax.axis_index(REQ)
    request_ids = jnp.arange(requests, dtype=jnp.int32)

    own_kv = key_value
    width = own_kv.shape[2]
    seg_rows = -(-tok_rows // width)
    seg_flat = jnp.pad(segment, (0, seg_rows * width - tok_rows)).astype(jnp.bfloat16)
    packed = jnp.concatenate(
        [own_kv.reshape(2 * tok_rows, width), seg_flat.reshape(seg_rows, width)], axis=0
    )
    parts_kv, parts_seg = [], []
    for back in range(REACH, 0, -1):
        got = from_behind(packed, REQ, back)
        parts_kv.append(got[: 2 * tok_rows].reshape(own_kv.shape))
        parts_seg.append(got[2 * tok_rows :].reshape(-1)[:tok_rows].astype(jnp.int32))
    parts_kv.append(own_kv)
    parts_seg.append(segment)
    next_first = from_behind(segment[:1], REQ, -1)
    window = jnp.concatenate(parts_kv, axis=1)
    seg_window = jnp.concatenate(parts_seg, axis=0)
    span = window.shape[1]
    key_index_i = (device - REACH) * tok_rows + jnp.arange(span, dtype=jnp.int32)
    valid = key_index_i >= 0
    same = (seg_window[:, None] == seg_window[None, :]) & valid[None, :]
    start_i = jnp.min(jnp.where(same, key_index_i[None, :], jnp.int32(2**30)), axis=1)
    key_index = key_index_i.astype(jnp.float32)
    win_start = start_i.astype(jnp.float32)
    win_pos = key_index - win_start
    own_start = win_start[span - tok_rows:]
    tok_index = key_index[span - tok_rows:]
    positions = win_pos[span - tok_rows:]

    cosine, sine_table = rope_tables(win_pos, HD)
    rot_keys = rotate(
        window[0].astype(jnp.float32).reshape(span, heads_kv, HD), cosine, sine_table
    ).astype(jnp.bfloat16)
    q_cos, q_sin = cosine[span - tok_rows:], sine_table[span - tok_rows:]
    rot_query = rotate(
        queries.astype(jnp.float32).reshape(tok_rows, heads_kv, GROUP, HD), q_cos, q_sin
    ).astype(jnp.bfloat16)
    key_cache = rot_keys[span - tok_rows:].reshape(tok_rows, heads_kv * HD)
    key_rows = rot_keys
    value_rows = window[1].reshape(span, heads_kv, HD)
    q_seg = segment
    allowed = (
        (seg_window[None, :] == q_seg[:, None])
        & valid[None, :]
        & (key_index[None, :] <= tok_index[:, None])
    )
    scale = HD ** (-0.5)
    scores_part = (
        jnp.einsum("qhgd,khd->hgqk", rot_query, key_rows, preferred_element_type=jnp.float32)
        * scale
    )
    scores = jnp.where(allowed[None, None], scores_part, masked_score)
    peak = jnp.max(scores, axis=3, keepdims=True)
    weights = jnp.exp(scores - peak)
    total = jnp.sum(weights, axis=3)
    context = jnp.einsum(
        "hgqk,khd->qhgd",
        weights.astype(jnp.bfloat16),
        value_rows,
        preferred_element_type=jnp.float32,
    )
    context = context / jnp.transpose(total, (2, 0, 1))[..., None]
    attended = context.astype(jnp.bfloat16).reshape(tok_rows, heads_kv * GROUP * HD)
    following = jnp.concatenate([segment[1:], next_first])
    is_last_dev = device == devices_req - 1
    is_end = following != segment
    is_end = is_end.at[tok_rows - 1].set(is_end[tok_rows - 1] | is_last_dev)
    select = (is_end[:, None] & (segment[:, None] == request_ids[None, :])).astype(jnp.bfloat16)
    end_rows = lax.dot_general(
        select,
        jnp.concatenate([attended, residual], axis=1),
        (((0,), (0,)), ((), ())),
        preferred_element_type=jnp.float32,
    ).astype(jnp.bfloat16)
    end_rows = butterfly(end_rows, REQ, jnp.add)
    attended, end_rows = lax.optimization_barrier((attended, end_rows))
    end_att, end_res = end_rows[:, : attended.shape[1]], end_rows[:, attended.shape[1] :]

    groups = lax.axis_size("tp")
    chip_half = lax.all_gather(out_weight, ("z", "x"), axis=1, tiled=True)
    halves = lax.all_gather(chip_half, "c", axis=0, tiled=False)
    cores, k_rows = halves.shape[0], halves.shape[1]
    per_group = halves.shape[2] // (groups * out_weight.shape[1])
    halves = halves.reshape(cores, k_rows, groups, per_group, out_weight.shape[1])
    both = jnp.einsum(
        "tk,ckgin->gticn",
        jnp.concatenate([attended, end_att], axis=0),
        halves,
        preferred_element_type=jnp.float32,
    ).astype(jnp.bfloat16)
    both = both.reshape(groups, both.shape[1], -1)
    end_part = both[:, tok_rows:]
    end_sum = halving_scatter(end_part, "tp")
    both, end_sum = lax.optimization_barrier((both, end_sum))
    own_share = lax.psum_scatter(both, "tp", scatter_dimension=0, tiled=True)[0, :tok_rows]
    own_share = own_share.astype(jnp.float32)
    hidden = (residual.astype(jnp.float32) + own_share).astype(jnp.bfloat16)
    last_state = (end_res.astype(jnp.float32) + end_sum).astype(jnp.bfloat16).astype(jnp.float32)
    scaled = (last_state * head_gain.astype(jnp.float32)).astype(jnp.bfloat16)
    square_part = jnp.sum(last_state * last_state, axis=1)
    logit_part = jnp.dot(scaled, vocab_weight, preferred_element_type=jnp.float32)
    summed = butterfly(
        jnp.concatenate([logit_part, square_part[:, None]], axis=1).astype(jnp.bfloat16), "tp", jnp.add
    ).astype(jnp.float32)
    raw_logits, square_sum = summed[:, :-1], summed[:, -1]
    mean_square = square_sum / D
    last_norm = jnp.sqrt(mean_square)
    local_top = jnp.max(raw_logits * lax.rsqrt(mean_square + eps)[:, None], axis=1)
    top_logit = butterfly(local_top, REQ, jnp.maximum)
    return (hidden, key_cache, last_norm, top_logit)


def solution(mesh):
    req_size = mesh.shape["req"]
    split = Mesh(mesh.devices.reshape(req_size // 8, 4, 2, mesh.shape["tp"]), REQ + ("tp",))
    placed = (
        P(REQ, "tp"),
        P(None, REQ, "tp"),
        P(REQ),
        P(REQ, "tp"),
        P("tp", REQ),
        P("tp"),
        P("tp", REQ),
    )
    return jax.shard_map(
        local,
        mesh=split,
        in_specs=placed,
        out_specs=(P(REQ, "tp"), P(REQ, "tp"), P(), P()),
        check_vma=False,
    )
```

```python
import jax
import jax.numpy as jnp
from jax import lax
from jax.sharding import PartitionSpec as P

D = 7168
HD = 128
GROUP = 7
REACH = 4


theta = 5000000.0
eps = 1e-05
masked_score = -1e30


def from_behind(value, axis, steps):
    count = lax.axis_size(axis)
    initial, last = (max(0, -steps), min(count, count - steps))
    return lax.ppermute(value, axis, [(source, source + steps) for source in range(initial, last)])


def butterfly(value, axis, combine):
    count = lax.axis_size(axis)
    stride = 1
    while stride < count:
        other = lax.ppermute(value, axis, [(source, source ^ stride) for source in range(count)])
        value = combine(value, other)
        stride *= 2
    return value


def halving_scatter(value, axis):
    count = lax.axis_size(axis)
    index = lax.axis_index(axis)
    rows, width = value.shape[1], value.shape[2]
    held = jnp.moveaxis(value, 0, 1)
    bit = 1
    while bit < count:
        mine = (index // bit) % 2
        pairs = held.reshape(rows, held.shape[1] // 2, 2, width)
        keep = lax.dynamic_index_in_dim(pairs, mine, 2, keepdims=False)
        give = lax.dynamic_index_in_dim(pairs, 1 - mine, 2, keepdims=False)
        moved = lax.ppermute(give, axis, [(source, source ^ bit) for source in range(count)])
        held = (keep.astype(jnp.float32) + moved.astype(jnp.float32)).astype(value.dtype)
        bit *= 2
    return held.reshape(rows, width).astype(jnp.float32)


def rope_tables(positions, width):
    half_width = width // 2
    frequency = theta ** (-(jnp.arange(half_width, dtype=jnp.float32) * 2.0 / width))
    angles = positions[:, None] * frequency[None, :]
    return (jnp.cos(angles), jnp.sin(angles))


def rotate(values, cosine, sine_table):
    half_width = values.shape[-1] // 2
    first_half = values[..., :half_width]
    second_half = values[..., half_width:]
    table_shape = (cosine.shape[0],) + (1,) * (values.ndim - 2) + (half_width,)
    cosine = cosine.reshape(table_shape)
    sine_table = sine_table.reshape(table_shape)
    return jnp.concatenate(
        [
            first_half * cosine - second_half * sine_table,
            second_half * cosine + first_half * sine_table,
        ],
        axis=-1,
    )


def local(queries, key_value, segment, residual, out_weight, head_gain, vocab_weight):
    tok_rows = segment.shape[0]
    heads_kv = key_value.shape[2] // HD
    requests = lax.axis_size("req") // 2
    devices_req = lax.axis_size("req")
    device = lax.axis_index("req")
    request_ids = jnp.arange(requests, dtype=jnp.int32)

    own_kv = key_value
    width = own_kv.shape[2]
    seg_rows = -(-tok_rows // width)
    seg_flat = jnp.pad(segment, (0, seg_rows * width - tok_rows)).astype(jnp.bfloat16)
    packed = jnp.concatenate(
        [own_kv.reshape(2 * tok_rows, width), seg_flat.reshape(seg_rows, width)], axis=0
    )
    parts_kv, parts_seg = [], []
    for back in range(REACH, 0, -1):
        got = from_behind(packed, "req", back)
        parts_kv.append(got[: 2 * tok_rows].reshape(own_kv.shape))
        parts_seg.append(got[2 * tok_rows :].reshape(-1)[:tok_rows].astype(jnp.int32))
    parts_kv.append(own_kv)
    parts_seg.append(segment)
    window = jnp.concatenate(parts_kv, axis=1)
    seg_window = jnp.concatenate(parts_seg, axis=0)
    span = window.shape[1]
    key_index_i = (device - REACH) * tok_rows + jnp.arange(span, dtype=jnp.int32)
    valid = key_index_i >= 0
    same = (seg_window[:, None] == seg_window[None, :]) & valid[None, :]
    start_i = jnp.min(jnp.where(same, key_index_i[None, :], jnp.int32(2**30)), axis=1)
    key_index = key_index_i.astype(jnp.float32)
    win_start = start_i.astype(jnp.float32)
    win_pos = key_index - win_start
    own_start = win_start[span - tok_rows:]
    tok_index = key_index[span - tok_rows:]
    positions = win_pos[span - tok_rows:]

    cosine, sine_table = rope_tables(win_pos, HD)
    rot_keys = rotate(
        window[0].astype(jnp.float32).reshape(span, heads_kv, HD), cosine, sine_table
    ).astype(jnp.bfloat16)
    q_cos, q_sin = cosine[span - tok_rows:], sine_table[span - tok_rows:]
    rot_query = rotate(
        queries.astype(jnp.float32).reshape(tok_rows, heads_kv, GROUP, HD), q_cos, q_sin
    ).astype(jnp.bfloat16)
    key_cache = rot_keys[span - tok_rows:].reshape(tok_rows, heads_kv * HD)
    key_rows = rot_keys
    value_rows = window[1].reshape(span, heads_kv, HD)
    q_seg = segment
    allowed = (
        (seg_window[None, :] == q_seg[:, None])
        & valid[None, :]
        & (key_index[None, :] <= tok_index[:, None])
    )
    scale = HD ** (-0.5)
    scores_part = (
        jnp.einsum("qhgd,khd->hgqk", rot_query, key_rows, preferred_element_type=jnp.float32)
        * scale
    )
    scores = jnp.where(allowed[None, None], scores_part, masked_score)
    peak = jnp.max(scores, axis=3, keepdims=True)
    weights = jnp.exp(scores - peak)
    total = jnp.sum(weights, axis=3)
    context = jnp.einsum(
        "hgqk,khd->qhgd",
        weights.astype(jnp.bfloat16),
        value_rows,
        preferred_element_type=jnp.float32,
    )
    context = context / jnp.transpose(total, (2, 0, 1))[..., None]
    attended = context.astype(jnp.bfloat16).reshape(tok_rows, heads_kv * GROUP * HD)
    is_end = jnp.concatenate([segment[1:] != segment[:-1], jnp.ones((1,), bool)])
    select = (is_end[:, None] & (segment[:, None] == request_ids[None, :])).astype(jnp.bfloat16)
    held = jnp.any(segment[:, None] == request_ids[None, :], axis=0)
    tag = jnp.where(held, device, -1).astype(jnp.bfloat16)
    end_rows = lax.dot_general(
        select,
        jnp.concatenate([attended, residual], axis=1),
        (((0,), (0,)), ((), ())),
        preferred_element_type=jnp.float32,
    ).astype(jnp.bfloat16)
    end_rows = jnp.concatenate([end_rows, tag[:, None]], axis=1)

    def latest(mine, other):
        return jnp.where(other[:, -1:] > mine[:, -1:], other, mine)

    end_rows = butterfly(end_rows, "req", latest)[:, :-1]
    attended, end_rows = lax.optimization_barrier((attended, end_rows))
    end_att, end_res = end_rows[:, : attended.shape[1]], end_rows[:, attended.shape[1] :]

    full_weight = lax.all_gather(out_weight, "req", axis=1, tiled=True)
    groups = lax.axis_size("tp")
    both = jnp.einsum(
        "tk,kgn->gtn",
        jnp.concatenate([attended, end_att], axis=0),
        full_weight.reshape(full_weight.shape[0], groups, -1),
        preferred_element_type=jnp.float32,
    ).astype(jnp.bfloat16)
    end_part = both[:, tok_rows:]
    end_sum = halving_scatter(end_part, "tp")
    both, end_sum = lax.optimization_barrier((both, end_sum))
    own_share = lax.psum_scatter(both, "tp", scatter_dimension=0, tiled=True)[0, :tok_rows]
    own_share = own_share.astype(jnp.float32)
    hidden = (residual.astype(jnp.float32) + own_share).astype(jnp.bfloat16)
    last_state = (end_res.astype(jnp.float32) + end_sum).astype(jnp.bfloat16).astype(jnp.float32)
    scaled = (last_state * head_gain.astype(jnp.float32)).astype(jnp.bfloat16)
    square_part = jnp.sum(last_state * last_state, axis=1)
    logit_part = jnp.dot(scaled, vocab_weight, preferred_element_type=jnp.float32)
    summed = butterfly(
        jnp.concatenate([logit_part, square_part[:, None]], axis=1).astype(jnp.bfloat16), "tp", jnp.add
    ).astype(jnp.float32)
    raw_logits, square_sum = summed[:, :-1], summed[:, -1]
    mean_square = square_sum / D
    last_norm = jnp.sqrt(mean_square)
    local_top = jnp.max(raw_logits * lax.rsqrt(mean_square + eps)[:, None], axis=1)
    top_logit = butterfly(local_top, "req", jnp.maximum)
    return (hidden, key_cache, last_norm, top_logit)


def solution(mesh):
    placed = (
        P("req", "tp"),
        P(None, "req", "tp"),
        P("req"),
        P("req", "tp"),
        P("tp", "req"),
        P("tp"),
        P("tp", "req"),
    )
    return jax.shard_map(
        local,
        mesh=mesh,
        in_specs=placed,
        out_specs=(P("req", "tp"), P("req", "tp"), P(), P()),
        check_vma=False,
    )
```
